128 devices in a mesh: dp: 8 (over y_lo, x), ctx: 16 (over z, y_hi, core).
Axes of the slice: x: 4, y: 4 (y_hi: 2, y_lo: 2; y = y_hi * 2 + y_lo), z: 4, core: 2. Of those that a mesh axis runs over, the one named last changes fastest.
Arguments:
- stream: bfloat16 [32768, 2, 1024], P(('dp', 'ctx')), parts along dimension 0, may hold values from -6 to 6
- w_gate: bfloat16 [1024, 2048], replicated, may hold values from -0.1875 to 0.1875
- w_xbc: bfloat16 [1024, 2176], replicated, may hold values from -0.1875 to 0.1875
- w_dt: bfloat16 [1024, 32], replicated, may hold values from -0.1875 to 0.1875
- dt_bias: float32 [2, 32], replicated, may hold values from -1 to 1
- decay_log: float32 [2, 32], replicated, may hold values from -16 to -3, as said below
- conv_w: float32 [2, 4, 2176], replicated, may hold values from -3 to 3
- conv_b: float32 [2, 2176], replicated, may hold values from -3 to 3
- skip_gain: float32 [2, 32], replicated, may hold values from 0.5 to 1.5
- norm_gain: float32 [2048], replicated, may hold values from 0.1 to 1.9
- w_out: bfloat16 [2048, 1024], replicated, may hold values from -0.125 to 0.125
Outputs:
- mixed: bfloat16 [32768, 2, 1024], P(('dp', 'ctx')), parts along dimension 0
The draws below stay inside these ranges and needn't reach their ends.
There are 8 independent parts, one for each index of `dp`. The reference program is written for one: setup_inputs(seed, part) draws one part's arguments, and reference() takes and returns one part's arrays. A program takes and returns all parts, laid end to end along the dimension named above; an argument that names none is the same for every part. Nothing has to cross between parts.
Inputs may be any that keep to these rules, and one draw needn't show every extreme that they name: `decay_log`: logarithms of per-step decay rates, one row per direction.
All inputs are finite; a program needn't handle non-finite values.
Results may differ from the reference program's by a relative error of at most 0.0095.
Values may be sent and summed in bfloat16 or wider, within the bound.
No kernel may reach another device: no remote copies, remote signals or barrier semaphores. Data moves between devices by JAX's collectives and lax.ppermute only.
A program may use at most 256 MiB of HBM per device.

```python
import math
import jax
import jax.numpy as jnp
from jax import lax

D = 1024
E = 2048
NS = 64
K = 4
Q = 256
H = 32
TOKENS = 4096


def draw_decay_log(key, part):
    uniform_part = jax.random.uniform(key, (2, H), jnp.float32)
    slow_end = math.log(0.02 / TOKENS)
    fast_end = math.log(0.03)
    return slow_end + (fast_end - slow_end) * uniform_part


def block_scale(key, shape, cuts, least, high):
    loudness, own = 1.0, jax.random.fold_in(key, 6)
    for dim, parts in cuts:
        steps = jnp.exp(jax.random.uniform(jax.random.fold_in(own, dim), (parts,), jnp.float32, least / len(cuts), high / len(cuts)))
        loudness = loudness * jnp.repeat(steps, shape[dim] // parts).reshape([-1 if axis == dim else 1 for axis in range(len(shape))])
    return loudness


def noise(stream_key, dims, width, bound, split=(), held_as=jnp.bfloat16):
    loudness = block_scale(stream_key, dims, split, -0.22, 0.18) if split else 1.0
    drawn = jax.random.normal(stream_key, dims, jnp.float32) * width * loudness
    return jnp.minimum(jnp.maximum(drawn, -bound), bound).astype(held_as)


def setup_inputs(seed: int = 0, part: int = 0) -> dict:
    arg_keys = jax.random.split(jax.random.key(seed), 12)
    own_keys = jax.random.split(jax.random.fold_in(arg_keys[11], part), 12)
    return {
        "stream": noise(own_keys[0], (TOKENS, 2, D), 1.0, 6.0, ((0, 16),)),
        "w_gate": noise(arg_keys[1], (D, E), D ** -0.5, 0.1875),
        "w_xbc": noise(arg_keys[2], (D, E + 2 * NS), D ** -0.5, 0.1875),
        "w_dt": noise(arg_keys[3], (D, H), D ** -0.5, 0.1875),
        "dt_bias": jnp.clip(jax.random.uniform(arg_keys[4], (2, H), jnp.float32, -1.0, 1.0), -1.0, 1.0),
        "decay_log": draw_decay_log(jax.random.fold_in(arg_keys[11], 71), part),
        "conv_w": noise(arg_keys[6], (2, K, E + 2 * NS), K ** -0.5, 3.0, (), jnp.float32),
        "conv_b": noise(arg_keys[7], (2, E + 2 * NS), 0.5, 3.0, (), jnp.float32),
        "skip_gain": jnp.clip(jax.random.uniform(arg_keys[8], (2, H), jnp.float32, 0.5, 1.5), 0.5, 1.5),
        "norm_gain": jnp.clip(1.0 + 0.18 * jax.random.normal(arg_keys[9], (E,), jnp.float32), 0.1, 1.9),
        "w_out": noise(arg_keys[10], (E, D), E ** -0.5, 0.125),
    }


def conv_rows(window, weights, offset):
    count = window.shape[0] - weights.shape[0] + 1
    total = offset[None, :] + weights[0][None, :] * window[0:count].astype(jnp.float32)
    for tap_index in range(1, weights.shape[0]):
        total = total + weights[tap_index][None, :] * window[tap_index:tap_index + count].astype(jnp.float32)
    return jax.nn.silu(total).astype(jnp.bfloat16)

def span_terms(conv_out, dt_raw, dt_shift, log_rate, skip_heads):
    length = conv_out.shape[0]
    heads = dt_raw.shape[1]
    inner = conv_out.shape[1] - 2 * NS
    head_size = inner // heads
    blocks = length // Q
    values = conv_out[:, :inner].reshape(blocks, Q, heads, head_size)
    keys_in = conv_out[:, inner:inner + NS].reshape(blocks, Q, NS)
    reads = conv_out[:, inner + NS:].reshape(blocks, Q, NS)
    step_sizes = jax.nn.softplus(dt_raw.astype(jnp.float32) + dt_shift[None, :]).reshape(blocks, Q, heads)
    rate = -jnp.exp(log_rate)
    cumulative = jnp.cumsum(step_sizes * rate[None, None, :], axis=1)
    by_head = jnp.transpose(cumulative, (0, 2, 1))
    lower = jnp.arange(Q)[:, None] >= jnp.arange(Q)[None, :]
    decay = jnp.exp(jnp.where(lower[None, None], by_head[:, :, :, None] - by_head[:, :, None, :], -1e+30))
    scores = jnp.einsum('cqn,csn->cqs', reads.astype(jnp.float32), keys_in.astype(jnp.float32), precision=lax.Precision.HIGHEST)
    mixing = (scores[:, None] * decay).astype(jnp.bfloat16)
    scaled = (values.astype(jnp.float32) * step_sizes[..., None]).astype(jnp.bfloat16)
    diagonal = jnp.einsum('chqs,cshp->cqhp', mixing.astype(jnp.float32), scaled.astype(jnp.float32), precision=lax.Precision.HIGHEST)
    to_end = jnp.exp(cumulative[:, -1:, :] - cumulative)
    weighted = (values.astype(jnp.float32) * (step_sizes * to_end)[..., None]).astype(jnp.bfloat16)
    block_states = jnp.einsum('cqhp,cqn->chpn', weighted.astype(jnp.float32), keys_in.astype(jnp.float32), precision=lax.Precision.HIGHEST)
    block_decay = jnp.exp(cumulative[:, -1, :])
    local_part = diagonal + skip_heads[None, None, :, None] * values.astype(jnp.float32)
    return (local_part, block_states, block_decay, cumulative, reads)

def carried(reads, cumulative, entering):
    product = jnp.einsum('cqn,chpn->cqhp', reads.astype(jnp.float32), entering, precision=lax.Precision.HIGHEST)
    return product * jnp.exp(cumulative)[..., None]

def one_direction(window, dt_raw, dt_shift, log_rate, weights, offset, skip_heads):
    conv_out = conv_rows(window, weights, offset)
    local_part, block_states, block_decay, cumulative, reads = span_terms(conv_out, dt_raw, dt_shift, log_rate, skip_heads)

    def advance(carry_state, item):
        piece_state, piece_decay = item
        return (piece_decay[:, None, None] * carry_state + piece_state, carry_state)
    start_state = jnp.zeros(block_states.shape[1:], jnp.float32)
    _, entering = lax.scan(advance, start_state, (block_states, block_decay))
    result = local_part + carried(reads, cumulative, entering)
    return result.reshape(result.shape[0] * result.shape[1], -1)

def mixer(strand_rows, params):
    w_gate, w_xbc, w_dt, dt_bias, decay_log, conv_w, conv_b, skip_gain, norm_gain, w_out = params
    gate = jnp.dot(strand_rows, w_gate, preferred_element_type=jnp.float32).astype(jnp.bfloat16)
    projected = jnp.dot(strand_rows, w_xbc, preferred_element_type=jnp.float32).astype(jnp.bfloat16)
    dt_raw = jnp.dot(strand_rows, w_dt, preferred_element_type=jnp.float32).astype(jnp.bfloat16)
    margin = jnp.zeros((K - 1, projected.shape[1]), jnp.bfloat16)
    ahead = one_direction(jnp.concatenate([margin, projected], axis=0), dt_raw, dt_bias[0], decay_log[0], conv_w[0], conv_b[0], skip_gain[0])
    behind = one_direction(jnp.concatenate([margin, projected[::-1]], axis=0), dt_raw[::-1], dt_bias[1], decay_log[1], conv_w[1], conv_b[1], skip_gain[1])[::-1]
    combined = ahead + behind
    gated = combined * jax.nn.silu(gate.astype(jnp.float32))
    normed = (gated * lax.rsqrt(lax.optimization_barrier(jnp.mean(gated * gated, axis=-1, keepdims=True)) + 1e-05) * norm_gain[None, :]).astype(jnp.bfloat16)
    return jnp.dot(normed, w_out, preferred_element_type=jnp.float32)

def reference(stream, w_gate, w_xbc, w_dt, dt_bias, decay_log, conv_w, conv_b, skip_gain, norm_gain, w_out):
    params = (w_gate, w_xbc, w_dt, dt_bias, decay_log, conv_w, conv_b, skip_gain, norm_gain, w_out)
    forward_rows = stream[:, 0, :]
    reverse_rows = stream[:, 1, :]
    first = (forward_rows.astype(jnp.float32) + mixer(forward_rows, params)).astype(jnp.bfloat16)
    second = (reverse_rows.astype(jnp.float32) + mixer(reverse_rows[::-1], params)[::-1]).astype(jnp.bfloat16)
    return jnp.stack([first, second], axis=1)
```

```python
import jax
import jax.numpy as jnp
from jax import lax
from jax.sharding import PartitionSpec as P

NS = 64
K = 4
Q = 256


def shifted(value, distance):
    size = lax.axis_size("ctx")
    if abs(distance) >= size:
        return jax.tree.map(jnp.zeros_like, value)
    if distance > 0:
        pairs = [(i, i + distance) for i in range(size - distance)]
    else:
        pairs = [(i - distance, i) for i in range(size + distance)]
    return lax.ppermute(value, "ctx", pairs)


def combine(earlier, later):
    return (earlier[0] * later[0], later[0][..., None, None] * earlier[1] + later[1])


def exclusive_chain(element, sense):
    size = lax.axis_size("ctx")
    cover = 1
    gathered = element
    while 2 * cover < size:
        gathered = combine(shifted(gathered, sense * cover), gathered)
        cover *= 2
    near = shifted(gathered, sense)
    far = shifted(gathered, sense * (cover + 1))
    return combine(far, near)[1]


def group_terms(window, dt_raw, dt_shift, log_rate, weights, offset, skip_heads, falling):
    runs, length = dt_raw.shape[0], dt_raw.shape[1]
    heads = dt_raw.shape[2]
    if falling:
        taps = [window[:, K - 1 - k : K - 1 - k + length] for k in range(K)]
    else:
        taps = [window[:, k : k + length] for k in range(K)]
    total = offset[:, None, :] + weights[:, 0][:, None, :] * taps[0].astype(jnp.float32)
    for k in range(1, K):
        total = total + weights[:, k][:, None, :] * taps[k].astype(jnp.float32)
    conv = jax.nn.silu(total).astype(jnp.bfloat16)
    inner = conv.shape[2] - 2 * NS
    head_size = inner // heads
    values = conv[:, :, :inner].reshape(runs, length, heads, head_size)
    keys_in = conv[:, :, inner : inner + NS]
    reads = conv[:, :, inner + NS :]
    step = jax.nn.softplus(dt_raw.astype(jnp.float32) + dt_shift[:, None, :])
    rate = -jnp.exp(log_rate)
    cum = lax.cumsum(step * rate[:, None, :], axis=1, reverse=falling)
    by_head = jnp.transpose(cum, (0, 2, 1))
    rows = jnp.arange(length)
    if falling:
        keep = rows[:, None] <= rows[None, :]
    else:
        keep = rows[:, None] >= rows[None, :]
    decay = jnp.exp(
        jnp.where(keep[None, None], by_head[:, :, :, None] - by_head[:, :, None, :], -1e30)
    )
    scores = jnp.einsum("rtn,rsn->rts", reads, keys_in, preferred_element_type=jnp.float32)
    mixing = (scores[:, None] * decay).astype(jnp.bfloat16)
    values32 = values.astype(jnp.float32)
    scaled = (values32 * step[..., None]).astype(jnp.bfloat16)
    diagonal = jnp.einsum("rhts,rshp->rthp", mixing, scaled, preferred_element_type=jnp.float32)
    last = cum[:, 0] if falling else cum[:, -1]
    to_end = jnp.exp(last[:, None, :] - cum)
    weighted = (values32 * (step * to_end)[..., None]).astype(jnp.bfloat16)
    block_state = jnp.einsum(
        "rshp,rsn->rhpn", weighted, keys_in, preferred_element_type=jnp.float32
    )
    block_decay = jnp.exp(last)
    local = diagonal + skip_heads[:, None, :, None] * values32
    return local, cum, reads, (block_decay, block_state)


def finish(local, cum, reads, entering):
    product = jnp.einsum(
        "rtn,rhpn->rthp", reads.astype(jnp.float32), entering, precision=lax.Precision.HIGHEST
    )
    result = local + product * jnp.exp(cum)[..., None]
    return result.reshape(result.shape[0], result.shape[1], -1)


def body(
    stream, w_gate, w_xbc, w_dt, dt_bias, decay_log, conv_w, conv_b, skip_gain, norm_gain, w_out
):
    length = stream.shape[0]
    rows = jnp.concatenate([stream[:, 0, :], stream[:, 1, :]], axis=0)
    gate = jnp.dot(rows, w_gate, preferred_element_type=jnp.float32).astype(jnp.bfloat16)
    projected = jnp.dot(rows, w_xbc, preferred_element_type=jnp.float32).astype(jnp.bfloat16)
    projected = projected.reshape(2, length, projected.shape[1])
    dt_raw = jnp.dot(rows, w_dt, preferred_element_type=jnp.float32).astype(jnp.bfloat16)
    dt_raw = dt_raw.reshape(2, length, dt_raw.shape[1])
    before = shifted(projected[:, length - (K - 1) :], 1)
    after = shifted(projected[:, : K - 1], -1)
    rising = group_terms(
        jnp.concatenate([before, projected], axis=1),
        dt_raw,
        dt_bias,
        decay_log,
        conv_w,
        conv_b,
        skip_gain,
        False,
    )
    falling = group_terms(
        jnp.concatenate([projected, after], axis=1),
        dt_raw,
        dt_bias[::-1],
        decay_log[::-1],
        conv_w[::-1],
        conv_b[::-1],
        skip_gain[::-1],
        True,
    )
    rising_in = exclusive_chain(rising[3], 1)
    falling_in = exclusive_chain(falling[3], -1)
    combined = finish(*rising[:3], rising_in) + finish(*falling[:3], falling_in)
    gated = combined * jax.nn.silu(gate.reshape(2, length, gate.shape[1]).astype(jnp.float32))
    normed = (
        gated * lax.rsqrt(jnp.mean(gated * gated, axis=-1, keepdims=True) + 1e-05) * norm_gain
    ).astype(jnp.bfloat16)
    projected_out = jnp.dot(
        normed.reshape(2 * length, normed.shape[2]), w_out, preferred_element_type=jnp.float32
    )
    final_rows = (rows.astype(jnp.float32) + projected_out).astype(jnp.bfloat16)
    return jnp.stack([final_rows[:length], final_rows[length:]], axis=1)


def solution(mesh):
    placed = (P(("dp", "ctx"), None, None), P(), P(), P(), P(), P(), P(), P(), P(), P(), P())
    return jax.shard_map(
        body, mesh=mesh, in_specs=placed, out_specs=P(("dp", "ctx"), None, None), check_vma=False
    )
```

```python
import jax
import jax.numpy as jnp
from jax import lax
from jax.sharding import PartitionSpec as P

NS = 64
K = 4
Q = 256
DECAY_LANES = 128


def shifted(value, distance):
    size = lax.axis_size("ctx")
    if abs(distance) >= size:
        return jax.tree.map(jnp.zeros_like, value)
    if distance > 0:
        pairs = [(i, i + distance) for i in range(size - distance)]
    else:
        pairs = [(i - distance, i) for i in range(size + distance)]
    return lax.ppermute(value, "ctx", pairs)


def combine(earlier, later):
    width = later.shape[-1] - DECAY_LANES
    lanes = lax.broadcasted_iota(jnp.int32, later.shape, later.ndim - 1)
    return later[..., width : width + 1] * earlier + jnp.where(lanes < width, later, 0.0)


def exclusive_chain(element, sense):
    size = lax.axis_size("ctx")
    cover = 1
    gathered = element
    while 2 * cover < size:
        gathered = combine(shifted(gathered, sense * cover), gathered)
        cover *= 2
    near = shifted(gathered, sense)
    far = shifted(gathered, sense * (cover + 1))
    chained = combine(far, near)
    return chained[..., : chained.shape[-1] - DECAY_LANES]


def group_terms(window, dt_raw, dt_shift, log_rate, weights, offset, skip_heads, falling):
    runs, length = dt_raw.shape[0], dt_raw.shape[1]
    heads = dt_raw.shape[2]
    if falling:
        taps = [window[:, K - 1 - k : K - 1 - k + length] for k in range(K)]
    else:
        taps = [window[:, k : k + length] for k in range(K)]
    total = offset[:, None, :] + weights[:, 0][:, None, :] * taps[0].astype(jnp.float32)
    for k in range(1, K):
        total = total + weights[:, k][:, None, :] * taps[k].astype(jnp.float32)
    conv = jax.nn.silu(total).astype(jnp.bfloat16)
    inner = conv.shape[2] - 2 * NS
    head_size = inner // heads
    values = conv[:, :, :inner].reshape(runs, length, heads, head_size)
    keys_in = conv[:, :, inner : inner + NS]
    reads = conv[:, :, inner + NS :]
    step = jax.nn.softplus(dt_raw.astype(jnp.float32) + dt_shift[:, None, :])
    rate = -jnp.exp(log_rate)
    cum = lax.cumsum(step * rate[:, None, :], axis=1, reverse=falling)
    by_head = jnp.transpose(cum, (0, 2, 1))
    rows = jnp.arange(length)
    if falling:
        keep = rows[:, None] <= rows[None, :]
    else:
        keep = rows[:, None] >= rows[None, :]
    decay = jnp.exp(
        jnp.where(keep[None, None], by_head[:, :, :, None] - by_head[:, :, None, :], -1e30)
    )
    scores = jnp.einsum("rtn,rsn->rts", reads, keys_in, preferred_element_type=jnp.float32)
    mixing = (scores[:, None] * decay).astype(jnp.bfloat16)
    values32 = values.astype(jnp.float32)
    scaled = (values32 * step[..., None]).astype(jnp.bfloat16)
    diagonal = jnp.einsum("rhts,rshp->rthp", mixing, scaled, preferred_element_type=jnp.float32)
    last = cum[:, 0] if falling else cum[:, -1]
    to_end = jnp.exp(last[:, None, :] - cum)
    weighted = (values32 * (step * to_end)[..., None]).astype(jnp.bfloat16)
    block_state = jnp.einsum(
        "rshp,rsn->rhpn", weighted, keys_in, preferred_element_type=jnp.float32
    )
    block_decay = jnp.exp(last)
    message = jnp.concatenate(
        [
            block_state.reshape(runs, heads, head_size * NS),
            jnp.broadcast_to(block_decay[..., None], (runs, heads, DECAY_LANES)),
        ],
        axis=-1,
    )
    local = diagonal + skip_heads[:, None, :, None] * values32
    return local, cum, reads, message


def finish(local, cum, reads, entering):
    entering = entering.reshape(local.shape[0], local.shape[2], local.shape[3], NS)
    product = jnp.einsum(
        "rtn,rhpn->rthp", reads.astype(jnp.float32), entering, precision=lax.Precision.HIGHEST
    )
    result = local + product * jnp.exp(cum)[..., None]
    return result.reshape(result.shape[0], result.shape[1], -1)


def body(
    stream, w_gate, w_xbc, w_dt, dt_bias, decay_log, conv_w, conv_b, skip_gain, norm_gain, w_out
):
    length = stream.shape[0]
    rows = jnp.concatenate([stream[:, 0, :], stream[:, 1, :]], axis=0)
    gate = jnp.dot(rows, w_gate, preferred_element_type=jnp.float32).astype(jnp.bfloat16)
    projected = jnp.dot(rows, w_xbc, preferred_element_type=jnp.float32).astype(jnp.bfloat16)
    projected = projected.reshape(2, length, projected.shape[1])
    dt_raw = jnp.dot(rows, w_dt, preferred_element_type=jnp.float32).astype(jnp.bfloat16)
    dt_raw = dt_raw.reshape(2, length, dt_raw.shape[1])
    before = shifted(projected[:, length - (K - 1) :], 1)
    after = shifted(projected[:, : K - 1], -1)
    rising = group_terms(
        jnp.concatenate([before, projected], axis=1),
        dt_raw,
        dt_bias,
        decay_log,
        conv_w,
        conv_b,
        skip_gain,
        False,
    )
    falling = group_terms(
        jnp.concatenate([projected, after], axis=1),
        dt_raw,
        dt_bias[::-1],
        decay_log[::-1],
        conv_w[::-1],
        conv_b[::-1],
        skip_gain[::-1],
        True,
    )
    rising_in = exclusive_chain(rising[3], 1)
    falling_in = exclusive_chain(falling[3], -1)
    combined = finish(*rising[:3], rising_in) + finish(*falling[:3], falling_in)
    gated = combined * jax.nn.silu(gate.reshape(2, length, gate.shape[1]).astype(jnp.float32))
    normed = (
        gated * lax.rsqrt(jnp.mean(gated * gated, axis=-1, keepdims=True) + 1e-05) * norm_gain
    ).astype(jnp.bfloat16)
    projected_out = jnp.dot(
        normed.reshape(2 * length, normed.shape[2]), w_out, preferred_element_type=jnp.float32
    )
    final_rows = (rows.astype(jnp.float32) + projected_out).astype(jnp.bfloat16)
    return jnp.stack([final_rows[:length], final_rows[length:]], axis=1)


def solution(mesh):
    placed = (P(("dp", "ctx"), None, None), P(), P(), P(), P(), P(), P(), P(), P(), P(), P())
    return jax.shard_map(
        body, mesh=mesh, in_specs=placed, out_specs=P(("dp", "ctx"), None, None), check_vma=False
    )
```

```python
import jax
import jax.numpy as jnp
from jax import lax
from jax.sharding import PartitionSpec as P

NS = 64
K = 4
Q = 256
DECAY_LANES = 128


def shifted(value, distance):
    size = lax.axis_size("ctx")
    if abs(distance) >= size:
        return jax.tree.map(jnp.zeros_like, value)
    if distance > 0:
        pairs = [(i, i + distance) for i in range(size - distance)]
    else:
        pairs = [(i - distance, i) for i in range(size + distance)]
    return lax.ppermute(value, "ctx", pairs)


def combine(earlier, later):
    width = later.shape[-1] - DECAY_LANES
    lanes = lax.broadcasted_iota(jnp.int32, later.shape, later.ndim - 1)
    return later[..., width : width + 1] * earlier + jnp.where(lanes < width, later, 0.0)


def exclusive_chain(element, sense):
    size = lax.axis_size("ctx")
    group = 4
    assert size == group * group
    here = lax.axis_index("ctx")
    spot = here if sense == 1 else size - 1 - here
    slot = spot % group

    def place(position):
        return position if sense == 1 else size - 1 - position

    def send(value, moves):
        return lax.ppermute(value, "ctx", [(place(a), place(b)) for a, b in moves])

    tops = range(0, size, group)
    first = send(element, [(t + k, t + k + 1) for t in tops for k in (0, 2)])
    pair = combine(first, element)
    other = send(pair, [(t + a, t + b) for t in tops for a, b in ((1, 3), (3, 1))])
    whole = jnp.where(slot == 1, combine(pair, other), combine(other, pair))
    ends = [t + k for t in tops for k in (1, 3)]
    previous = send(whole, [(a, a + group) for a in ends if a + group < size])
    two = combine(previous, whole)
    further = send(two, [(a, a + 2 * group) for a in ends if a + 2 * group < size])
    entering = combine(further, previous)
    handed = jnp.where(slot == 1, entering, combine(entering, other))
    below = send(handed, [(t + k + 1, t + k) for t in tops for k in (0, 2)])
    chained = jnp.where(slot % 2 == 1, combine(handed, first), below)
    return chained[..., : chained.shape[-1] - DECAY_LANES]


def group_terms(window, dt_raw, dt_shift, log_rate, weights, offset, skip_heads, falling):
    runs, length = dt_raw.shape[0], dt_raw.shape[1]
    heads = dt_raw.shape[2]
    if falling:
        taps = [window[:, K - 1 - k : K - 1 - k + length] for k in range(K)]
    else:
        taps = [window[:, k : k + length] for k in range(K)]
    total = offset[:, None, :] + weights[:, 0][:, None, :] * taps[0].astype(jnp.float32)
    for k in range(1, K):
        total = total + weights[:, k][:, None, :] * taps[k].astype(jnp.float32)
    conv = jax.nn.silu(total).astype(jnp.bfloat16)
    inner = conv.shape[2] - 2 * NS
    head_size = inner // heads
    values = conv[:, :, :inner].reshape(runs, length, heads, head_size)
    keys_in = conv[:, :, inner : inner + NS]
    reads = conv[:, :, inner + NS :]
    step = jax.nn.softplus(dt_raw.astype(jnp.float32) + dt_shift[:, None, :])
    rate = -jnp.exp(log_rate)
    cum = lax.cumsum(step * rate[:, None, :], axis=1, reverse=falling)
    by_head = jnp.transpose(cum, (0, 2, 1))
    rows = jnp.arange(length)
    if falling:
        keep = rows[:, None] <= rows[None, :]
    else:
        keep = rows[:, None] >= rows[None, :]
    decay = jnp.exp(
        jnp.where(keep[None, None], by_head[:, :, :, None] - by_head[:, :, None, :], -1e30)
    )
    scores = jnp.einsum("rtn,rsn->rts", reads, keys_in, preferred_element_type=jnp.float32)
    mixing = (scores[:, None] * decay).astype(jnp.bfloat16)
    values32 = values.astype(jnp.float32)
    scaled = (values32 * step[..., None]).astype(jnp.bfloat16)
    diagonal = jnp.einsum("rhts,rshp->rthp", mixing, scaled, preferred_element_type=jnp.float32)
    last = cum[:, 0] if falling else cum[:, -1]
    to_end = jnp.exp(last[:, None, :] - cum)
    weighted = (values32 * (step * to_end)[..., None]).astype(jnp.bfloat16)
    block_state = jnp.einsum(
        "rshp,rsn->rhpn", weighted, keys_in, preferred_element_type=jnp.float32
    )
    block_decay = jnp.exp(last)
    message = jnp.concatenate(
        [
            block_state.reshape(runs, heads, head_size * NS),
            jnp.broadcast_to(block_decay[..., None], (runs, heads, DECAY_LANES)),
        ],
        axis=-1,
    )
    local = diagonal + skip_heads[:, None, :, None] * values32
    return local, cum, reads, message


def finish(local, cum, reads, entering):
    entering = entering.reshape(local.shape[0], local.shape[2], local.shape[3], NS)
    product = jnp.einsum(
        "rtn,rhpn->rthp", reads.astype(jnp.float32), entering, precision=lax.Precision.HIGHEST
    )
    result = local + product * jnp.exp(cum)[..., None]
    return result.reshape(result.shape[0], result.shape[1], -1)


def body(
    stream, w_gate, w_xbc, w_dt, dt_bias, decay_log, conv_w, conv_b, skip_gain, norm_gain, w_out
):
    length = stream.shape[0]
    rows = jnp.concatenate([stream[:, 0, :], stream[:, 1, :]], axis=0)
    gate = jnp.dot(rows, w_gate, preferred_element_type=jnp.float32).astype(jnp.bfloat16)
    projected = jnp.dot(rows, w_xbc, preferred_element_type=jnp.float32).astype(jnp.bfloat16)
    projected = projected.reshape(2, length, projected.shape[1])
    dt_raw = jnp.dot(rows, w_dt, preferred_element_type=jnp.float32).astype(jnp.bfloat16)
    dt_raw = dt_raw.reshape(2, length, dt_raw.shape[1])
    before = shifted(projected[:, length - (K - 1) :], 1)
    after = shifted(projected[:, : K - 1], -1)
    rising = group_terms(
        jnp.concatenate([before, projected], axis=1),
        dt_raw,
        dt_bias,
        decay_log,
        conv_w,
        conv_b,
        skip_gain,
        False,
    )
    falling = group_terms(
        jnp.concatenate([projected, after], axis=1),
        dt_raw,
        dt_bias[::-1],
        decay_log[::-1],
        conv_w[::-1],
        conv_b[::-1],
        skip_gain[::-1],
        True,
    )
    rising_in = exclusive_chain(rising[3], 1)
    falling_in = exclusive_chain(falling[3], -1)
    combined = finish(*rising[:3], rising_in) + finish(*falling[:3], falling_in)
    gated = combined * jax.nn.silu(gate.reshape(2, length, gate.shape[1]).astype(jnp.float32))
    normed = (
        gated * lax.rsqrt(jnp.mean(gated * gated, axis=-1, keepdims=True) + 1e-05) * norm_gain
    ).astype(jnp.bfloat16)
    projected_out = jnp.dot(
        normed.reshape(2 * length, normed.shape[2]), w_out, preferred_element_type=jnp.float32
    )
    final_rows = (rows.astype(jnp.float32) + projected_out).astype(jnp.bfloat16)
    return jnp.stack([final_rows[:length], final_rows[length:]], axis=1)


def solution(mesh):
    placed = (P(("dp", "ctx"), None, None), P(), P(), P(), P(), P(), P(), P(), P(), P(), P())
    return jax.shard_map(
        body, mesh=mesh, in_specs=placed, out_specs=P(("dp", "ctx"), None, None), check_vma=False
    )
```

```python
import jax
import jax.numpy as jnp
from jax import lax
from jax.sharding import PartitionSpec as P

NS = 64
K = 4
Q = 256
DECAY_LANES = 128


def shifted(value, distance):
    size = lax.axis_size("ctx")
    if abs(distance) >= size:
        return jax.tree.map(jnp.zeros_like, value)
    if distance > 0:
        pairs = [(i, i + distance) for i in range(size - distance)]
    else:
        pairs = [(i - distance, i) for i in range(size + distance)]
    return lax.ppermute(value, "ctx", pairs)


def combine(earlier, later):
    width = later.shape[-1] - DECAY_LANES
    lanes = lax.broadcasted_iota(jnp.int32, later.shape, later.ndim - 1)
    return later[..., width : width + 1] * earlier + jnp.where(lanes < width, later, 0.0)


def exclusive_chain(element, sense):
    size = lax.axis_size("ctx")
    group = 4
    assert size == group * group
    here = lax.axis_index("ctx")
    spot = here if sense == 1 else size - 1 - here
    slot = spot % group

    def place(position):
        return position if sense == 1 else size - 1 - position

    def send(value, moves):
        pairs = [(place(a), place(b)) for a, b in moves]
        moved = lax.ppermute(value.astype(jnp.bfloat16), "ctx", pairs)
        return moved.astype(jnp.float32)

    tops = range(0, size, group)
    first = send(element, [(t + k, t + k + 1) for t in tops for k in (0, 2)])
    pair = combine(first, element)
    other = send(pair, [(t + a, t + b) for t in tops for a, b in ((1, 3), (3, 1))])
    whole = jnp.where(slot == 1, combine(pair, other), combine(other, pair))
    ends = [t + k for t in tops for k in (1, 3)]
    previous = send(whole, [(a, a + group) for a in ends if a + group < size])
    two = combine(previous, whole)
    further = send(two, [(a, a + 2 * group) for a in ends if a + 2 * group < size])
    entering = combine(further, previous)
    handed = jnp.where(slot == 1, entering, combine(entering, other))
    below = send(handed, [(t + k + 1, t + k) for t in tops for k in (0, 2)])
    chained = jnp.where(slot % 2 == 1, combine(handed, first), below)
    return chained[..., : chained.shape[-1] - DECAY_LANES]


def group_terms(window, dt_raw, dt_shift, log_rate, weights, offset, skip_heads, falling):
    runs, length = dt_raw.shape[0], dt_raw.shape[1]
    heads = dt_raw.shape[2]
    if falling:
        taps = [window[:, K - 1 - k : K - 1 - k + length] for k in range(K)]
    else:
        taps = [window[:, k : k + length] for k in range(K)]
    total = offset[:, None, :] + weights[:, 0][:, None, :] * taps[0].astype(jnp.float32)
    for k in range(1, K):
        total = total + weights[:, k][:, None, :] * taps[k].astype(jnp.float32)
    conv = jax.nn.silu(total).astype(jnp.bfloat16)
    inner = conv.shape[2] - 2 * NS
    head_size = inner // heads
    values = conv[:, :, :inner].reshape(runs, length, heads, head_size)
    keys_in = conv[:, :, inner : inner + NS]
    reads = conv[:, :, inner + NS :]
    step = jax.nn.softplus(dt_raw.astype(jnp.float32) + dt_shift[:, None, :])
    rate = -jnp.exp(log_rate)
    cum = lax.cumsum(step * rate[:, None, :], axis=1, reverse=falling)
    by_head = jnp.transpose(cum, (0, 2, 1))
    rows = jnp.arange(length)
    if falling:
        keep = rows[:, None] <= rows[None, :]
    else:
        keep = rows[:, None] >= rows[None, :]
    decay = jnp.exp(
        jnp.where(keep[None, None], by_head[:, :, :, None] - by_head[:, :, None, :], -1e30)
    )
    scores = jnp.einsum("rtn,rsn->rts", reads, keys_in, preferred_element_type=jnp.float32)
    mixing = (scores[:, None] * decay).astype(jnp.bfloat16)
    values32 = values.astype(jnp.float32)
    scaled = (values32 * step[..., None]).astype(jnp.bfloat16)
    diagonal = jnp.einsum("rhts,rshp->rthp", mixing, scaled, preferred_element_type=jnp.float32)
    last = cum[:, 0] if falling else cum[:, -1]
    to_end = jnp.exp(last[:, None, :] - cum)
    weighted = (values32 * (step * to_end)[..., None]).astype(jnp.bfloat16)
    block_state = jnp.einsum(
        "rshp,rsn->rhpn", weighted, keys_in, preferred_element_type=jnp.float32
    )
    block_decay = jnp.exp(last)
    message = jnp.concatenate(
        [
            block_state.reshape(runs, heads, head_size * NS),
            jnp.broadcast_to(block_decay[..., None], (runs, heads, DECAY_LANES)),
        ],
        axis=-1,
    )
    local = diagonal + skip_heads[:, None, :, None] * values32
    return local, cum, reads, message


def finish(local, cum, reads, entering):
    entering = entering.reshape(local.shape[0], local.shape[2], local.shape[3], NS)
    product = jnp.einsum(
        "rtn,rhpn->rthp", reads.astype(jnp.float32), entering, precision=lax.Precision.HIGHEST
    )
    result = local + product * jnp.exp(cum)[..., None]
    return result.reshape(result.shape[0], result.shape[1], -1)


def body(
    stream, w_gate, w_xbc, w_dt, dt_bias, decay_log, conv_w, conv_b, skip_gain, norm_gain, w_out
):
    length = stream.shape[0]
    rows = jnp.concatenate([stream[:, 0, :], stream[:, 1, :]], axis=0)
    gate = jnp.dot(rows, w_gate, preferred_element_type=jnp.float32).astype(jnp.bfloat16)
    projected = jnp.dot(rows, w_xbc, preferred_element_type=jnp.float32).astype(jnp.bfloat16)
    projected = projected.reshape(2, length, projected.shape[1])
    dt_raw = jnp.dot(rows, w_dt, preferred_element_type=jnp.float32).astype(jnp.bfloat16)
    dt_raw = dt_raw.reshape(2, length, dt_raw.shape[1])
    before = shifted(projected[:, length - (K - 1) :], 1)
    after = shifted(projected[:, : K - 1], -1)
    rising = group_terms(
        jnp.concatenate([before, projected], axis=1),
        dt_raw,
        dt_bias,
        decay_log,
        conv_w,
        conv_b,
        skip_gain,
        False,
    )
    falling = group_terms(
        jnp.concatenate([projected, after], axis=1),
        dt_raw,
        dt_bias[::-1],
        decay_log[::-1],
        conv_w[::-1],
        conv_b[::-1],
        skip_gain[::-1],
        True,
    )
    rising_in = exclusive_chain(rising[3], 1)
    falling_in = exclusive_chain(falling[3], -1)
    combined = finish(*rising[:3], rising_in) + finish(*falling[:3], falling_in)
    gated = combined * jax.nn.silu(gate.reshape(2, length, gate.shape[1]).astype(jnp.float32))
    normed = (
        gated * lax.rsqrt(jnp.mean(gated * gated, axis=-1, keepdims=True) + 1e-05) * norm_gain
    ).astype(jnp.bfloat16)
    projected_out = jnp.dot(
        normed.reshape(2 * length, normed.shape[2]), w_out, preferred_element_type=jnp.float32
    )
    final_rows = (rows.astype(jnp.float32) + projected_out).astype(jnp.bfloat16)
    return jnp.stack([final_rows[:length], final_rows[length:]], axis=1)


def solution(mesh):
    placed = (P(("dp", "ctx"), None, None), P(), P(), P(), P(), P(), P(), P(), P(), P(), P())
    return jax.shard_map(
        body, mesh=mesh, in_specs=placed, out_specs=P(("dp", "ctx"), None, None), check_vma=False
    )
```

```python
import jax
import jax.numpy as jnp
from jax import lax
from jax.sharding import PartitionSpec as P

NS = 64
K = 4
Q = 256
DECAY_LANES = 128


def shifted(value, distance):
    size = lax.axis_size("ctx")
    if abs(distance) >= size:
        return jax.tree.map(jnp.zeros_like, value)
    if distance > 0:
        pairs = [(i, i + distance) for i in range(size - distance)]
    else:
        pairs = [(i - distance, i) for i in range(size + distance)]
    return lax.ppermute(value, "ctx", pairs)


def combine(earlier, later):
    width = later.shape[-1] - DECAY_LANES
    lanes = lax.broadcasted_iota(jnp.int32, later.shape, later.ndim - 1)
    return later[..., width : width + 1] * earlier + jnp.where(lanes < width, later, 0.0)


def exclusive_chain(element, sense):
    size = lax.axis_size("ctx")
    group = 4
    assert size == group * group
    here = lax.axis_index("ctx")
    spot = here if sense == 1 else size - 1 - here
    slot = spot % group

    def place(position):
        return position if sense == 1 else size - 1 - position

    def send(value, moves):
        pairs = [(place(a), place(b)) for a, b in moves]
        moved = lax.ppermute(value.astype(jnp.bfloat16), "ctx", pairs)
        return moved.astype(jnp.float32)

    tops = range(0, size, group)
    first = send(element, [(t + k, t + k + 1) for t in tops for k in (0, 2)])
    pair = combine(first, element)
    other = send(pair, [(t + a, t + b) for t in tops for a, b in ((1, 3), (3, 1))])
    whole = jnp.where(slot == 1, combine(pair, other), combine(other, pair))
    ends = [t + k for t in tops for k in (1, 3)]
    previous = send(whole, [(a, a + group) for a in ends if a + group < size])
    two = combine(previous, whole)
    further = send(two, [(a, a + 2 * group) for a in ends if a + 2 * group < size])
    entering = combine(further, previous)
    handed = jnp.where(slot == 1, entering, combine(entering, other))
    below = send(handed, [(t + k + 1, t + k) for t in tops for k in (0, 2)])
    chained = jnp.where(slot % 2 == 1, combine(handed, first), below)
    return chained[..., : chained.shape[-1] - DECAY_LANES]


def group_terms(window, dt_raw, dt_shift, log_rate, weights, offset, skip_heads, falling):
    runs, length = dt_raw.shape[0], dt_raw.shape[1]
    heads = dt_raw.shape[2]
    if falling:
        taps = [window[:, K - 1 - k : K - 1 - k + length] for k in range(K)]
    else:
        taps = [window[:, k : k + length] for k in range(K)]
    total = offset[:, None, :] + weights[:, 0][:, None, :] * taps[0].astype(jnp.float32)
    for k in range(1, K):
        total = total + weights[:, k][:, None, :] * taps[k].astype(jnp.float32)
    conv = jax.nn.silu(total).astype(jnp.bfloat16)
    inner = conv.shape[2] - 2 * NS
    head_size = inner // heads
    values = conv[:, :, :inner].reshape(runs, length, heads, head_size)
    keys_in = conv[:, :, inner : inner + NS]
    reads = conv[:, :, inner + NS :]
    step = jax.nn.softplus(dt_raw.astype(jnp.float32) + dt_shift[:, None, :])
    rate = -jnp.exp(log_rate)
    cum = lax.cumsum(step * rate[:, None, :], axis=1, reverse=falling)
    by_head = jnp.transpose(cum, (0, 2, 1))
    rows = jnp.arange(length)
    if falling:
        keep = rows[:, None] <= rows[None, :]
    else:
        keep = rows[:, None] >= rows[None, :]
    decay = jnp.exp(
        jnp.where(keep[None, None], by_head[:, :, :, None] - by_head[:, :, None, :], -1e30)
    )
    scores = jnp.einsum("rtn,rsn->rts", reads, keys_in, preferred_element_type=jnp.float32)
    mixing = (scores[:, None] * decay).astype(jnp.bfloat16)
    values32 = values.astype(jnp.float32)
    scaled = (values32 * step[..., None]).astype(jnp.bfloat16)
    diagonal = jnp.einsum("rhts,rshp->rthp", mixing, scaled, preferred_element_type=jnp.float32)
    last = cum[:, 0] if falling else cum[:, -1]
    to_end = jnp.exp(last[:, None, :] - cum)
    weighted = (values32 * (step * to_end)[..., None]).astype(jnp.bfloat16)
    block_state = jnp.einsum(
        "rshp,rsn->rhpn", weighted, keys_in, preferred_element_type=jnp.float32
    )
    block_decay = jnp.exp(last)
    message = jnp.concatenate(
        [
            block_state.reshape(runs, heads, head_size * NS),
            jnp.broadcast_to(block_decay[..., None], (runs, heads, DECAY_LANES)),
        ],
        axis=-1,
    )
    local = diagonal + skip_heads[:, None, :, None] * values32
    return local, cum, reads, message


def finish(local, cum, reads, entering):
    entering = entering.reshape(local.shape[0], local.shape[2], local.shape[3], NS)
    product = jnp.einsum(
        "rtn,rhpn->rthp", reads.astype(jnp.float32), entering, precision=lax.Precision.HIGHEST
    )
    return local + product * jnp.exp(cum)[..., None]


def swapped(pair):
    return jnp.concatenate([pair[1:2], pair[0:1]], axis=0)


def body(
    stream, w_gate, w_xbc, w_dt, dt_bias, decay_log, conv_w, conv_b, skip_gain, norm_gain, w_out
):
    length = stream.shape[0]
    rows = jnp.concatenate([stream[:, 0, :], stream[:, 1, :]], axis=0)
    gate = jnp.dot(rows, w_gate, preferred_element_type=jnp.float32).astype(jnp.bfloat16)
    projected = jnp.dot(rows, w_xbc, preferred_element_type=jnp.float32).astype(jnp.bfloat16)
    projected = projected.reshape(2, length, projected.shape[1])
    dt_raw = jnp.dot(rows, w_dt, preferred_element_type=jnp.float32).astype(jnp.bfloat16)
    dt_raw = dt_raw.reshape(2, length, dt_raw.shape[1])
    before = shifted(projected[:, length - (K - 1) :], 1)
    after = shifted(projected[:, : K - 1], -1)
    rising = group_terms(
        jnp.concatenate([before, projected], axis=1),
        dt_raw,
        dt_bias,
        decay_log,
        conv_w,
        conv_b,
        skip_gain,
        False,
    )
    falling = group_terms(
        jnp.concatenate([projected, after], axis=1),
        dt_raw,
        swapped(dt_bias),
        swapped(decay_log),
        swapped(conv_w),
        swapped(conv_b),
        swapped(skip_gain),
        True,
    )
    rising_in = exclusive_chain(rising[3], 1)
    falling_in = exclusive_chain(falling[3], -1)
    combined = finish(*rising[:3], rising_in) + finish(*falling[:3], falling_in)
    heads, head_size = combined.shape[2], combined.shape[3]
    gate_heads = gate.reshape(2, length, heads, head_size).astype(jnp.float32)
    gated = combined * jax.nn.silu(gate_heads)
    mean_square = jnp.mean(gated * gated, axis=(2, 3), keepdims=True)
    normed = (
        gated * lax.rsqrt(mean_square + 1e-05) * norm_gain.reshape(heads, head_size)
    ).astype(jnp.bfloat16)
    projected_out = jnp.einsum(
        "rthp,hpd->rtd",
        normed,
        w_out.reshape(heads, head_size, w_out.shape[1]),
        preferred_element_type=jnp.float32,
    )
    final_rows = (rows.reshape(2, length, -1).astype(jnp.float32) + projected_out).astype(
        jnp.bfloat16
    )
    return jnp.stack([final_rows[0], final_rows[1]], axis=1)


def solution(mesh):
    placed = (P(("dp", "ctx"), None, None), P(), P(), P(), P(), P(), P(), P(), P(), P(), P())
    return jax.shard_map(
        body, mesh=mesh, in_specs=placed, out_specs=P(("dp", "ctx"), None, None), check_vma=False
    )
```

```python
import jax
import jax.numpy as jnp
from jax import lax
from jax.experimental.layout import Layout, with_layout_constraint
from jax.sharding import PartitionSpec as P

NS = 64
K = 4
Q = 256
DECAY_LANES = 128


def shifted(value, distance):
    size = lax.axis_size("ctx")
    if abs(distance) >= size:
        return jax.tree.map(jnp.zeros_like, value)
    if distance > 0:
        pairs = [(i, i + distance) for i in range(size - distance)]
    else:
        pairs = [(i - distance, i) for i in range(size + distance)]
    return lax.ppermute(value, "ctx", pairs)


def combine(earlier, later):
    width = later.shape[-1] - DECAY_LANES
    lanes = lax.broadcasted_iota(jnp.int32, later.shape, later.ndim - 1)
    return later[..., width : width + 1] * earlier + jnp.where(lanes < width, later, 0.0)


def exclusive_chain(element, sense):
    size = lax.axis_size("ctx")
    group = 4
    assert size == group * group
    here = lax.axis_index("ctx")
    spot = here if sense == 1 else size - 1 - here
    slot = spot % group

    def place(position):
        return position if sense == 1 else size - 1 - position

    def send(value, moves):
        pairs = [(place(a), place(b)) for a, b in moves]
        moved = lax.ppermute(value.astype(jnp.bfloat16), "ctx", pairs)
        return moved.astype(jnp.float32)

    tops = range(0, size, group)
    first = send(element, [(t + k, t + k + 1) for t in tops for k in (0, 2)])
    pair = combine(first, element)
    other = send(pair, [(t + a, t + b) for t in tops for a, b in ((1, 3), (3, 1))])
    whole = jnp.where(slot == 1, combine(pair, other), combine(other, pair))
    ends = [t + k for t in tops for k in (1, 3)]
    previous = send(whole, [(a, a + group) for a in ends if a + group < size])
    two = combine(previous, whole)
    further = send(two, [(a, a + 2 * group) for a in ends if a + 2 * group < size])
    entering = combine(further, previous)
    handed = jnp.where(slot == 1, entering, combine(entering, other))
    below = send(handed, [(t + k + 1, t + k) for t in tops for k in (0, 2)])
    chained = jnp.where(slot % 2 == 1, combine(handed, first), below)
    return chained[..., : chained.shape[-1] - DECAY_LANES]


def group_terms(window, dt_raw, dt_shift, log_rate, weights, offset, skip_heads, falling):
    runs, length = dt_raw.shape[0], dt_raw.shape[1]
    heads = dt_raw.shape[2]
    if falling:
        taps = [window[:, K - 1 - k : K - 1 - k + length] for k in range(K)]
    else:
        taps = [window[:, k : k + length] for k in range(K)]
    total = offset[:, None, :] + weights[:, 0][:, None, :] * taps[0].astype(jnp.float32)
    for k in range(1, K):
        total = total + weights[:, k][:, None, :] * taps[k].astype(jnp.float32)
    conv = with_layout_constraint(jax.nn.silu(total).astype(jnp.bfloat16), Layout((0, 1, 2)))
    inner = conv.shape[2] - 2 * NS
    head_size = inner // heads
    values = conv[:, :, :inner].reshape(runs, length, heads, head_size)
    keys_in = conv[:, :, inner : inner + NS]
    reads = conv[:, :, inner + NS :]
    step = jax.nn.softplus(dt_raw.astype(jnp.float32) + dt_shift[:, None, :])
    rate = -jnp.exp(log_rate)
    cum = lax.cumsum(step * rate[:, None, :], axis=1, reverse=falling)
    by_head = jnp.transpose(cum, (0, 2, 1))
    rows = jnp.arange(length)
    if falling:
        keep = rows[:, None] <= rows[None, :]
    else:
        keep = rows[:, None] >= rows[None, :]
    decay = jnp.exp(
        jnp.where(keep[None, None], by_head[:, :, :, None] - by_head[:, :, None, :], -1e30)
    )
    scores = jnp.einsum("rtn,rsn->rts", reads, keys_in, preferred_element_type=jnp.float32)
    mixing = (scores[:, None] * decay).astype(jnp.bfloat16)
    values32 = values.astype(jnp.float32)
    scaled = (values32 * step[..., None]).astype(jnp.bfloat16)
    diagonal = jnp.einsum("rhts,rshp->rthp", mixing, scaled, preferred_element_type=jnp.float32)
    last = cum[:, 0] if falling else cum[:, -1]
    to_end = jnp.exp(last[:, None, :] - cum)
    weighted = (values32 * (step * to_end)[..., None]).astype(jnp.bfloat16)
    block_state = jnp.einsum(
        "rshp,rsn->rhpn", weighted, keys_in, preferred_element_type=jnp.float32
    )
    block_decay = jnp.exp(last)
    message = jnp.concatenate(
        [
            block_state.reshape(runs, heads, head_size * NS),
            jnp.broadcast_to(block_decay[..., None], (runs, heads, DECAY_LANES)),
        ],
        axis=-1,
    )
    local = diagonal + skip_heads[:, None, :, None] * values32
    return local, cum, reads, message


def finish(local, cum, reads, entering):
    entering = entering.reshape(local.shape[0], local.shape[2], local.shape[3], NS)
    product = jnp.einsum(
        "rtn,rhpn->rthp", reads.astype(jnp.float32), entering, precision=lax.Precision.HIGHEST
    )
    return local + product * jnp.exp(cum)[..., None]


def swapped(pair):
    return jnp.concatenate([pair[1:2], pair[0:1]], axis=0)


def body(
    stream, w_gate, w_xbc, w_dt, dt_bias, decay_log, conv_w, conv_b, skip_gain, norm_gain, w_out
):
    length = stream.shape[0]
    rows = jnp.concatenate([stream[:, 0, :], stream[:, 1, :]], axis=0)
    gate = jnp.dot(rows, w_gate, preferred_element_type=jnp.float32).astype(jnp.bfloat16)
    projected = jnp.dot(rows, w_xbc, preferred_element_type=jnp.float32).astype(jnp.bfloat16)
    projected = projected.reshape(2, length, projected.shape[1])
    dt_raw = jnp.dot(rows, w_dt, preferred_element_type=jnp.float32).astype(jnp.bfloat16)
    dt_raw = dt_raw.reshape(2, length, dt_raw.shape[1])
    before = shifted(projected[:, length - (K - 1) :], 1)
    after = shifted(projected[:, : K - 1], -1)
    rising = group_terms(
        jnp.concatenate([before, projected], axis=1),
        dt_raw,
        dt_bias,
        decay_log,
        conv_w,
        conv_b,
        skip_gain,
        False,
    )
    falling = group_terms(
        jnp.concatenate([projected, after], axis=1),
        dt_raw,
        swapped(dt_bias),
        swapped(decay_log),
        swapped(conv_w),
        swapped(conv_b),
        swapped(skip_gain),
        True,
    )
    rising_in = exclusive_chain(rising[3], 1)
    falling_in = exclusive_chain(falling[3], -1)
    combined = finish(*rising[:3], rising_in) + finish(*falling[:3], falling_in)
    heads, head_size = combined.shape[2], combined.shape[3]
    gate_heads = gate.reshape(2, length, heads, head_size).astype(jnp.float32)
    gated = combined * jax.nn.silu(gate_heads)
    mean_square = jnp.mean(gated * gated, axis=(2, 3), keepdims=True)
    normed = (
        gated * lax.rsqrt(mean_square + 1e-05) * norm_gain.reshape(heads, head_size)
    ).astype(jnp.bfloat16)
    projected_out = jnp.einsum(
        "rthp,hpd->rtd",
        normed,
        w_out.reshape(heads, head_size, w_out.shape[1]),
        preferred_element_type=jnp.float32,
    )
    final_rows = (rows.reshape(2, length, -1).astype(jnp.float32) + projected_out).astype(
        jnp.bfloat16
    )
    return jnp.stack([final_rows[0], final_rows[1]], axis=1)


def solution(mesh):
    placed = (P(("dp", "ctx"), None, None), P(), P(), P(), P(), P(), P(), P(), P(), P(), P())
    return jax.shard_map(
        body, mesh=mesh, in_specs=placed, out_specs=P(("dp", "ctx"), None, None), check_vma=False
    )
```

```python
import jax
import jax.numpy as jnp
from jax import lax
from jax.sharding import PartitionSpec as P

NS = 64
K = 4
Q = 256
DECAY_LANES = 128


def shifted(value, distance):
    size = lax.axis_size("ctx")
    if abs(distance) >= size:
        return jax.tree.map(jnp.zeros_like, value)
    if distance > 0:
        pairs = [(i, i + distance) for i in range(size - distance)]
    else:
        pairs = [(i - distance, i) for i in range(size + distance)]
    return lax.ppermute(value, "ctx", pairs)


def combine(earlier, later):
    width = later.shape[-1] - DECAY_LANES
    lanes = lax.broadcasted_iota(jnp.int32, later.shape, later.ndim - 1)
    return later[..., width : width + 1] * earlier + jnp.where(lanes < width, later, 0.0)


def exclusive_chain(element, sense):
    size = lax.axis_size("ctx")
    group = 4
    assert size == group * group
    here = lax.axis_index("ctx")
    spot = here if sense == 1 else size - 1 - here
    slot = spot % group

    def place(position):
        return position if sense == 1 else size - 1 - position

    def send(value, moves):
        pairs = [(place(a), place(b)) for a, b in moves]
        moved = lax.ppermute(value.astype(jnp.bfloat16), "ctx", pairs)
        return moved.astype(jnp.float32)

    tops = range(0, size, group)
    first = send(element, [(t + k, t + k + 1) for t in tops for k in (0, 2)])
    pair = combine(first, element)
    other = send(pair, [(t + a, t + b) for t in tops for a, b in ((1, 3), (3, 1))])
    whole = jnp.where(slot == 1, combine(pair, other), combine(other, pair))
    ends = [t + k for t in tops for k in (1, 3)]
    previous = send(whole, [(a, a + group) for a in ends if a + group < size])
    two = combine(previous, whole)
    further = send(two, [(a, a + 2 * group) for a in ends if a + 2 * group < size])
    entering = combine(further, previous)
    handed = jnp.where(slot == 1, entering, combine(entering, other))
    below = send(handed, [(t + k + 1, t + k) for t in tops for k in (0, 2)])
    chained = jnp.where(slot % 2 == 1, combine(handed, first), below)
    return chained[..., : chained.shape[-1] - DECAY_LANES]


def group_terms(window, dt_raw, dt_shift, log_rate, weights, offset, skip_heads, falling):
    runs, length = dt_raw.shape[0], dt_raw.shape[1]
    heads = dt_raw.shape[2]
    if falling:
        taps = [window[:, K - 1 - k : K - 1 - k + length] for k in range(K)]
    else:
        taps = [window[:, k : k + length] for k in range(K)]
    total = offset[:, None, :] + weights[:, 0][:, None, :] * taps[0].astype(jnp.float32)
    for k in range(1, K):
        total = total + weights[:, k][:, None, :] * taps[k].astype(jnp.float32)
    conv = jax.nn.silu(total).astype(jnp.bfloat16)
    inner = conv.shape[2] - 2 * NS
    head_size = inner // heads
    values = conv[:, :, :inner].reshape(runs, length, heads, head_size)
    keys_in = conv[:, :, inner : inner + NS]
    reads = conv[:, :, inner + NS :]
    step = jax.nn.softplus(dt_raw.astype(jnp.float32) + dt_shift[:, None, :])
    rate = -jnp.exp(log_rate)
    rows = jnp.arange(length)
    if falling:
        keep = rows[:, None] <= rows[None, :]
    else:
        keep = rows[:, None] >= rows[None, :]
    cum = jnp.einsum(
        "ts,rsh->rth",
        keep.astype(jnp.float32),
        step * rate[:, None, :],
        precision=lax.Precision.HIGHEST,
    )
    by_head = jnp.transpose(cum, (0, 2, 1))
    decay = jnp.exp(
        jnp.where(keep[None, None], by_head[:, :, :, None] - by_head[:, :, None, :], -1e30)
    )
    scores = jnp.einsum("rtn,rsn->rts", reads, keys_in, preferred_element_type=jnp.float32)
    mixing = (scores[:, None] * decay).astype(jnp.bfloat16)
    values32 = values.astype(jnp.float32)
    scaled = (values32 * step[..., None]).astype(jnp.bfloat16)
    diagonal = jnp.einsum("rhts,rshp->rthp", mixing, scaled, preferred_element_type=jnp.float32)
    last = cum[:, 0] if falling else cum[:, -1]
    to_end = jnp.exp(last[:, None, :] - cum)
    weighted = (values32 * (step * to_end)[..., None]).astype(jnp.bfloat16)
    block_state = jnp.einsum(
        "rshp,rsn->rhpn", weighted, keys_in, preferred_element_type=jnp.float32
    )
    block_decay = jnp.exp(last)
    message = jnp.concatenate(
        [
            block_state.reshape(runs, heads, head_size * NS),
            jnp.broadcast_to(block_decay[..., None], (runs, heads, DECAY_LANES)),
        ],
        axis=-1,
    )
    local = diagonal + skip_heads[:, None, :, None] * values32
    return local, cum, reads, message


def finish(local, cum, reads, entering):
    entering = entering.reshape(local.shape[0], local.shape[2], local.shape[3], NS)
    product = jnp.einsum(
        "rtn,rhpn->rthp", reads.astype(jnp.float32), entering, precision=lax.Precision.HIGHEST
    )
    return local + product * jnp.exp(cum)[..., None]


def swapped(pair):
    return jnp.concatenate([pair[1:2], pair[0:1]], axis=0)


def body(
    stream, w_gate, w_xbc, w_dt, dt_bias, decay_log, conv_w, conv_b, skip_gain, norm_gain, w_out
):
    length = stream.shape[0]
    rows = jnp.concatenate([stream[:, 0, :], stream[:, 1, :]], axis=0)
    gate = jnp.dot(rows, w_gate, preferred_element_type=jnp.float32).astype(jnp.bfloat16)
    projected = jnp.dot(rows, w_xbc, preferred_element_type=jnp.float32).astype(jnp.bfloat16)
    projected = projected.reshape(2, length, projected.shape[1])
    dt_raw = jnp.dot(rows, w_dt, preferred_element_type=jnp.float32).astype(jnp.bfloat16)
    dt_raw = dt_raw.reshape(2, length, dt_raw.shape[1])
    before = shifted(projected[:, length - (K - 1) :], 1)
    after = shifted(projected[:, : K - 1], -1)
    rising = group_terms(
        jnp.concatenate([before, projected], axis=1),
        dt_raw,
        dt_bias,
        decay_log,
        conv_w,
        conv_b,
        skip_gain,
        False,
    )
    falling = group_terms(
        jnp.concatenate([projected, after], axis=1),
        dt_raw,
        swapped(dt_bias),
        swapped(decay_log),
        swapped(conv_w),
        swapped(conv_b),
        swapped(skip_gain),
        True,
    )
    rising_in = exclusive_chain(rising[3], 1)
    falling_in = exclusive_chain(falling[3], -1)
    combined = finish(*rising[:3], rising_in) + finish(*falling[:3], falling_in)
    heads, head_size = combined.shape[2], combined.shape[3]
    gate_heads = gate.reshape(2, length, heads, head_size).astype(jnp.float32)
    gated = combined * jax.nn.silu(gate_heads)
    mean_square = jnp.mean(gated * gated, axis=(2, 3), keepdims=True)
    normed = (
        gated * lax.rsqrt(mean_square + 1e-05) * norm_gain.reshape(heads, head_size)
    ).astype(jnp.bfloat16)
    projected_out = jnp.einsum(
        "rthp,hpd->rtd",
        normed,
        w_out.reshape(heads, head_size, w_out.shape[1]),
        preferred_element_type=jnp.float32,
    )
    final_rows = (rows.reshape(2, length, -1).astype(jnp.float32) + projected_out).astype(
        jnp.bfloat16
    )
    return jnp.stack([final_rows[0], final_rows[1]], axis=1)


def solution(mesh):
    placed = (P(("dp", "ctx"), None, None), P(), P(), P(), P(), P(), P(), P(), P(), P(), P())
    return jax.shard_map(
        body, mesh=mesh, in_specs=placed, out_specs=P(("dp", "ctx"), None, None), check_vma=False
    )
```

```python
import jax
import jax.numpy as jnp
from jax import lax
from jax.sharding import PartitionSpec as P

NS = 64
K = 4
Q = 256
DECAY_LANES = 128


def shifted(value, distance):
    size = lax.axis_size("ctx")
    if abs(distance) >= size:
        return jax.tree.map(jnp.zeros_like, value)
    if distance > 0:
        pairs = [(i, i + distance) for i in range(size - distance)]
    else:
        pairs = [(i - distance, i) for i in range(size + distance)]
    return lax.ppermute(value, "ctx", pairs)


def combine(earlier, later):
    width = later.shape[-1] - DECAY_LANES
    lanes = lax.broadcasted_iota(jnp.int32, later.shape, later.ndim - 1)
    return later[..., width : width + 1] * earlier + jnp.where(lanes < width, later, 0.0)


def exclusive_chain(element, sense):
    size = lax.axis_size("ctx")
    group = 4
    assert size == group * group
    here = lax.axis_index("ctx")
    spot = here if sense == 1 else size - 1 - here
    slot = spot % group

    def place(position):
        return position if sense == 1 else size - 1 - position

    def send(value, moves):
        pairs = [(place(a), place(b)) for a, b in moves]
        moved = lax.ppermute(value.astype(jnp.bfloat16), "ctx", pairs)
        return moved.astype(jnp.float32)

    tops = range(0, size, group)
    first = send(element, [(t + k, t + k + 1) for t in tops for k in (0, 2)])
    pair = combine(first, element)
    other = send(pair, [(t + a, t + b) for t in tops for a, b in ((1, 3), (3, 1))])
    whole = jnp.where(slot == 1, combine(pair, other), combine(other, pair))
    ends = [t + k for t in tops for k in (1, 3)]
    previous = send(whole, [(a, a + group) for a in ends if a + group < size])
    two = combine(previous, whole)
    further = send(two, [(a, a + 2 * group) for a in ends if a + 2 * group < size])
    entering = combine(further, previous)
    handed = jnp.where(slot == 1, entering, combine(entering, other))
    below = send(handed, [(t + k + 1, t + k) for t in tops for k in (0, 2)])
    chained = jnp.where(slot % 2 == 1, combine(handed, first), below)
    return chained[..., : chained.shape[-1] - DECAY_LANES]


def group_terms(window, dt_raw, dt_shift, log_rate, weights, offset, skip_heads, falling):
    runs, length = dt_raw.shape[0], dt_raw.shape[1]
    heads = dt_raw.shape[2]
    if falling:
        taps = [window[:, K - 1 - k : K - 1 - k + length] for k in range(K)]
    else:
        taps = [window[:, k : k + length] for k in range(K)]
    total = offset[:, None, :] + weights[:, 0][:, None, :] * taps[0].astype(jnp.float32)
    for k in range(1, K):
        total = total + weights[:, k][:, None, :] * taps[k].astype(jnp.float32)
    conv = jax.nn.silu(total).astype(jnp.bfloat16)
    inner = conv.shape[2] - 2 * NS
    head_size = inner // heads
    values = conv[:, :, :inner].reshape(runs, length, heads, head_size)
    keys_in = conv[:, :, inner : inner + NS]
    reads = conv[:, :, inner + NS :]
    step = jax.nn.softplus(dt_raw.astype(jnp.float32) + dt_shift[:, None, :])
    rate = -jnp.exp(log_rate)
    rows = jnp.arange(length)
    if falling:
        keep = rows[:, None] <= rows[None, :]
    else:
        keep = rows[:, None] >= rows[None, :]
    cum = jnp.einsum(
        "ts,rsh->rth",
        keep.astype(jnp.float32),
        step * rate[:, None, :],
        precision=lax.Precision.HIGHEST,
    )
    by_head = jnp.transpose(cum, (0, 2, 1))
    decay = jnp.exp(
        jnp.where(keep[None, None], by_head[:, :, :, None] - by_head[:, :, None, :], -1e30)
    )
    scores = jnp.einsum("rtn,rsn->rts", reads, keys_in, preferred_element_type=jnp.float32)
    mixing = (scores[:, None] * decay).astype(jnp.bfloat16)
    values32 = values.astype(jnp.float32)
    scaled = (values32 * step[..., None]).astype(jnp.bfloat16)
    diagonal = jnp.einsum("rhts,rshp->rthp", mixing, scaled, preferred_element_type=jnp.float32)
    last = cum[:, 0] if falling else cum[:, -1]
    to_end = jnp.exp(last[:, None, :] - cum)
    weighted = (values32 * (step * to_end)[..., None]).astype(jnp.bfloat16)
    block_state = jnp.einsum(
        "rshp,rsn->rhpn", weighted, keys_in, preferred_element_type=jnp.float32
    )
    block_decay = jnp.exp(last)
    message = jnp.concatenate(
        [
            block_state.reshape(runs, heads, head_size * NS),
            jnp.broadcast_to(block_decay[..., None], (runs, heads, DECAY_LANES)),
        ],
        axis=-1,
    )
    local = diagonal + skip_heads[:, None, :, None] * values32
    return local, cum, reads, message


def finish(local, cum, reads, entering):
    entering = entering.reshape(local.shape[0], local.shape[2], local.shape[3], NS)
    product = jnp.einsum(
        "rtn,rhpn->rthp", reads.astype(jnp.float32), entering, precision=lax.Precision.HIGHEST
    )
    return local + product * jnp.exp(cum)[..., None]


def swapped(pair):
    return jnp.concatenate([pair[1:2], pair[0:1]], axis=0)


def body(
    stream, w_gate, w_xbc, w_dt, dt_bias, decay_log, conv_w, conv_b, skip_gain, norm_gain, w_out
):
    length = stream.shape[0]
    rows = jnp.concatenate([stream[:, 0, :], stream[:, 1, :]], axis=0)
    gate = jnp.einsum(
        "rtd,de->ret", rows.reshape(2, length, -1), w_gate, preferred_element_type=jnp.float32
    ).astype(jnp.bfloat16)
    projected = jnp.dot(rows, w_xbc, preferred_element_type=jnp.float32).astype(jnp.bfloat16)
    projected = projected.reshape(2, length, projected.shape[1])
    dt_raw = jnp.dot(rows, w_dt, preferred_element_type=jnp.float32).astype(jnp.bfloat16)
    dt_raw = dt_raw.reshape(2, length, dt_raw.shape[1])
    before = shifted(projected[:, length - (K - 1) :], 1)
    after = shifted(projected[:, : K - 1], -1)
    rising = group_terms(
        jnp.concatenate([before, projected], axis=1),
        dt_raw,
        dt_bias,
        decay_log,
        conv_w,
        conv_b,
        skip_gain,
        False,
    )
    falling = group_terms(
        jnp.concatenate([projected, after], axis=1),
        dt_raw,
        swapped(dt_bias),
        swapped(decay_log),
        swapped(conv_w),
        swapped(conv_b),
        swapped(skip_gain),
        True,
    )
    rising_in = exclusive_chain(rising[3], 1)
    falling_in = exclusive_chain(falling[3], -1)
    combined = finish(*rising[:3], rising_in) + finish(*falling[:3], falling_in)
    heads, head_size = combined.shape[2], combined.shape[3]
    gate_heads = jnp.transpose(
        gate.reshape(2, heads, head_size, length).astype(jnp.float32), (0, 3, 1, 2)
    )
    gated = combined * jax.nn.silu(gate_heads)
    mean_square = jnp.mean(gated * gated, axis=(2, 3), keepdims=True)
    normed = (
        gated * lax.rsqrt(mean_square + 1e-05) * norm_gain.reshape(heads, head_size)
    ).astype(jnp.bfloat16)
    projected_out = jnp.einsum(
        "rthp,hpd->rtd",
        normed,
        w_out.reshape(heads, head_size, w_out.shape[1]),
        preferred_element_type=jnp.float32,
    )
    final_rows = (rows.reshape(2, length, -1).astype(jnp.float32) + projected_out).astype(
        jnp.bfloat16
    )
    return jnp.stack([final_rows[0], final_rows[1]], axis=1)


def solution(mesh):
    placed = (P(("dp", "ctx"), None, None), P(), P(), P(), P(), P(), P(), P(), P(), P(), P())
    return jax.shard_map(
        body, mesh=mesh, in_specs=placed, out_specs=P(("dp", "ctx"), None, None), check_vma=False
    )
```

```python
import jax
import jax.numpy as jnp
from jax import lax
from jax.sharding import PartitionSpec as P

NS = 64
K = 4
Q = 256
DECAY_LANES = 128


def shifted(value, distance):
    size = lax.axis_size("ctx")
    if abs(distance) >= size:
        return jax.tree.map(jnp.zeros_like, value)
    if distance > 0:
        pairs = [(i, i + distance) for i in range(size - distance)]
    else:
        pairs = [(i - distance, i) for i in range(size + distance)]
    return lax.ppermute(value, "ctx", pairs)


def combine(earlier, later):
    width = later.shape[-1] - DECAY_LANES
    lanes = lax.broadcasted_iota(jnp.int32, later.shape, later.ndim - 1)
    return later[..., width : width + 1] * earlier + jnp.where(lanes < width, later, 0.0)


def exclusive_chain(element, sense):
    size = lax.axis_size("ctx")
    group = 4
    assert size == group * group
    here = lax.axis_index("ctx")
    spot = here if sense == 1 else size - 1 - here
    slot = spot % group

    def place(position):
        return position if sense == 1 else size - 1 - position

    def send(value, moves):
        pairs = [(place(a), place(b)) for a, b in moves]
        moved = lax.ppermute(value.astype(jnp.bfloat16), "ctx", pairs)
        return moved.astype(jnp.float32)

    tops = range(0, size, group)
    first = send(element, [(t + k, t + k + 1) for t in tops for k in (0, 2)])
    pair = combine(first, element)
    other = send(pair, [(t + a, t + b) for t in tops for a, b in ((1, 3), (3, 1))])
    whole = jnp.where(slot == 1, combine(pair, other), combine(other, pair))
    ends = [t + k for t in tops for k in (1, 3)]
    previous = send(whole, [(a, a + group) for a in ends if a + group < size])
    two = combine(previous, whole)
    further = send(two, [(a, a + 2 * group) for a in ends if a + 2 * group < size])
    entering = combine(further, previous)
    handed = jnp.where(slot == 1, entering, combine(entering, other))
    below = send(handed, [(t + k + 1, t + k) for t in tops for k in (0, 2)])
    chained = jnp.where(slot % 2 == 1, combine(handed, first), below)
    return chained[..., : chained.shape[-1] - DECAY_LANES]


def group_terms(window, dt_raw, dt_shift, log_rate, weights, offset, skip_heads, falling):
    runs, length = dt_raw.shape[0], dt_raw.shape[1]
    heads = dt_raw.shape[2]
    window = window.astype(jnp.float32)
    if falling:
        taps = [window[:, K - 1 - k : K - 1 - k + length] for k in range(K)]
    else:
        taps = [window[:, k : k + length] for k in range(K)]
    total = offset[:, None, :] + weights[:, 0][:, None, :] * taps[0]
    for k in range(1, K):
        total = total + weights[:, k][:, None, :] * taps[k]
    conv = jax.nn.silu(total).astype(jnp.bfloat16)
    inner = conv.shape[2] - 2 * NS
    head_size = inner // heads
    values = conv[:, :, :inner].reshape(runs, length, heads, head_size)
    keys_in = conv[:, :, inner : inner + NS]
    reads = conv[:, :, inner + NS :]
    step = jax.nn.softplus(dt_raw.astype(jnp.float32) + dt_shift[:, None, :])
    rate = -jnp.exp(log_rate)
    rows = jnp.arange(length)
    if falling:
        keep = rows[:, None] <= rows[None, :]
    else:
        keep = rows[:, None] >= rows[None, :]
    cum = jnp.einsum(
        "ts,rsh->rth",
        keep.astype(jnp.float32),
        step * rate[:, None, :],
        precision=lax.Precision.HIGHEST,
    )
    by_head = jnp.transpose(cum, (0, 2, 1))
    decay = jnp.exp(
        jnp.where(keep[None, None], by_head[:, :, :, None] - by_head[:, :, None, :], -1e30)
    )
    scores = jnp.einsum("rtn,rsn->rts", reads, keys_in, preferred_element_type=jnp.float32)
    mixing = (scores[:, None] * decay).astype(jnp.bfloat16)
    values32 = values.astype(jnp.float32)
    scaled = (values32 * step[..., None]).astype(jnp.bfloat16)
    diagonal = jnp.einsum("rhts,rshp->rthp", mixing, scaled, preferred_element_type=jnp.float32)
    last = cum[:, 0] if falling else cum[:, -1]
    to_end = jnp.exp(last[:, None, :] - cum)
    weighted = (values32 * (step * to_end)[..., None]).astype(jnp.bfloat16)
    block_state = jnp.einsum(
        "rshp,rsn->rhpn", weighted, keys_in, preferred_element_type=jnp.float32
    )
    block_decay = jnp.exp(last)
    message = jnp.concatenate(
        [
            block_state.reshape(runs, heads, head_size * NS),
            jnp.broadcast_to(block_decay[..., None], (runs, heads, DECAY_LANES)),
        ],
        axis=-1,
    )
    local = diagonal + skip_heads[:, None, :, None] * values32
    return local, cum, reads, message


def finish(local, cum, reads, entering):
    entering = entering.reshape(local.shape[0], local.shape[2], local.shape[3], NS)
    product = jnp.einsum(
        "rtn,rhpn->rthp", reads.astype(jnp.float32), entering, precision=lax.Precision.HIGHEST
    )
    return local + product * jnp.exp(cum)[..., None]


def swapped(pair):
    return jnp.concatenate([pair[1:2], pair[0:1]], axis=0)


def body(
    stream, w_gate, w_xbc, w_dt, dt_bias, decay_log, conv_w, conv_b, skip_gain, norm_gain, w_out
):
    length = stream.shape[0]
    rows = jnp.concatenate([stream[:, 0, :], stream[:, 1, :]], axis=0)
    gate = jnp.einsum(
        "rtd,de->ret", rows.reshape(2, length, -1), w_gate, preferred_element_type=jnp.float32
    ).astype(jnp.bfloat16)
    projected = jnp.dot(rows, w_xbc, preferred_element_type=jnp.float32).astype(jnp.bfloat16)
    projected = projected.reshape(2, length, projected.shape[1])
    dt_raw = jnp.dot(rows, w_dt, preferred_element_type=jnp.float32).astype(jnp.bfloat16)
    dt_raw = dt_raw.reshape(2, length, dt_raw.shape[1])
    before = shifted(projected[:, length - (K - 1) :], 1)
    after = shifted(projected[:, : K - 1], -1)
    rising = group_terms(
        jnp.concatenate([before, projected], axis=1),
        dt_raw,
        dt_bias,
        decay_log,
        conv_w,
        conv_b,
        skip_gain,
        False,
    )
    falling = group_terms(
        jnp.concatenate([projected, after], axis=1),
        dt_raw,
        swapped(dt_bias),
        swapped(decay_log),
        swapped(conv_w),
        swapped(conv_b),
        swapped(skip_gain),
        True,
    )
    rising_in = exclusive_chain(rising[3], 1)
    falling_in = exclusive_chain(falling[3], -1)
    combined = finish(*rising[:3], rising_in) + finish(*falling[:3], falling_in)
    heads, head_size = combined.shape[2], combined.shape[3]
    gate_heads = jnp.transpose(
        gate.reshape(2, heads, head_size, length).astype(jnp.float32), (0, 3, 1, 2)
    )
    gated = combined * jax.nn.silu(gate_heads)
    mean_square = jnp.mean(gated * gated, axis=(2, 3), keepdims=True)
    normed = (
        gated * lax.rsqrt(mean_square + 1e-05) * norm_gain.reshape(heads, head_size)
    ).astype(jnp.bfloat16)
    projected_out = jnp.einsum(
        "rthp,hpd->rtd",
        normed,
        w_out.reshape(heads, head_size, w_out.shape[1]),
        preferred_element_type=jnp.float32,
    )
    final_rows = (rows.reshape(2, length, -1).astype(jnp.float32) + projected_out).astype(
        jnp.bfloat16
    )
    return jnp.stack([final_rows[0], final_rows[1]], axis=1)


def solution(mesh):
    placed = (P(("dp", "ctx"), None, None), P(), P(), P(), P(), P(), P(), P(), P(), P(), P())
    return jax.shard_map(
        body, mesh=mesh, in_specs=placed, out_specs=P(("dp", "ctx"), None, None), check_vma=False
    )
```

```python
import jax
import jax.numpy as jnp
from jax import lax
from jax.experimental import pallas as pl
from jax.experimental.pallas import tpu as pltpu
from jax.sharding import PartitionSpec as P

NS = 64
K = 4
Q = 256
DECAY_LANES = 128


def shifted(value, distance):
    size = lax.axis_size("ctx")
    if abs(distance) >= size:
        return jax.tree.map(jnp.zeros_like, value)
    if distance > 0:
        pairs = [(i, i + distance) for i in range(size - distance)]
    else:
        pairs = [(i - distance, i) for i in range(size + distance)]
    return lax.ppermute(value, "ctx", pairs)


def combine(earlier, later):
    width = later.shape[-1] - DECAY_LANES
    lanes = lax.broadcasted_iota(jnp.int32, later.shape, later.ndim - 1)
    return later[..., width : width + 1] * earlier + jnp.where(lanes < width, later, 0.0)


def exclusive_chain(element, sense):
    size = lax.axis_size("ctx")
    group = 4
    assert size == group * group
    here = lax.axis_index("ctx")
    spot = here if sense == 1 else size - 1 - here
    slot = spot % group

    def place(position):
        return position if sense == 1 else size - 1 - position

    def send(value, moves):
        pairs = [(place(a), place(b)) for a, b in moves]
        moved = lax.ppermute(value.astype(jnp.bfloat16), "ctx", pairs)
        return moved.astype(jnp.float32)

    tops = range(0, size, group)
    first = send(element, [(t + k, t + k + 1) for t in tops for k in (0, 2)])
    pair = combine(first, element)
    other = send(pair, [(t + a, t + b) for t in tops for a, b in ((1, 3), (3, 1))])
    whole = jnp.where(slot == 1, combine(pair, other), combine(other, pair))
    ends = [t + k for t in tops for k in (1, 3)]
    previous = send(whole, [(a, a + group) for a in ends if a + group < size])
    two = combine(previous, whole)
    further = send(two, [(a, a + 2 * group) for a in ends if a + 2 * group < size])
    entering = combine(further, previous)
    handed = jnp.where(slot == 1, entering, combine(entering, other))
    below = send(handed, [(t + k + 1, t + k) for t in tops for k in (0, 2)])
    chained = jnp.where(slot % 2 == 1, combine(handed, first), below)
    return chained[..., : chained.shape[-1] - DECAY_LANES]


def conv_kernel(x_ref, before_ref, after_ref, wr_ref, br_ref, wf_ref, bf_ref, rise_ref, fall_ref, pad):
    length = x_ref.shape[1]
    x = x_ref[0].astype(jnp.float32)
    pad[pl.ds(0, K - 1), :] = before_ref[0].astype(jnp.float32)
    pad[pl.ds(K - 1, length), :] = x
    total = br_ref[0] + wr_ref[0, 0:1, :] * pad[pl.ds(0, length), :]
    for k in range(1, K):
        total = total + wr_ref[0, k : k + 1, :] * pad[pl.ds(k, length), :]
    rise_ref[0] = jnp.transpose(jax.nn.silu(total)).astype(rise_ref.dtype)
    pad[pl.ds(0, length), :] = x
    pad[pl.ds(length, K - 1), :] = after_ref[0].astype(jnp.float32)
    total = bf_ref[0] + wf_ref[0, 0:1, :] * pad[pl.ds(K - 1, length), :]
    for k in range(1, K):
        total = total + wf_ref[0, k : k + 1, :] * pad[pl.ds(K - 1 - k, length), :]
    fall_ref[0] = jnp.transpose(jax.nn.silu(total)).astype(fall_ref.dtype)


def convolve(projected, before, after, w_rise, b_rise, w_fall, b_fall):
    runs, length, channels = projected.shape
    lanes = 128
    grid = (runs, channels // lanes)
    rows = lambda r, c: (r, 0, c)
    out_spec = pl.BlockSpec((1, lanes, length), lambda r, c: (r, c, 0))
    rise, fall = pl.pallas_call(
        conv_kernel,
        grid=grid,
        in_specs=[
            pl.BlockSpec((1, length, lanes), rows),
            pl.BlockSpec((1, K - 1, lanes), rows),
            pl.BlockSpec((1, K - 1, lanes), rows),
            pl.BlockSpec((1, K, lanes), rows),
            pl.BlockSpec((1, 1, lanes), rows),
            pl.BlockSpec((1, K, lanes), rows),
            pl.BlockSpec((1, 1, lanes), rows),
        ],
        out_specs=[out_spec, out_spec],
        out_shape=[jax.ShapeDtypeStruct((runs, channels, length), jnp.bfloat16)] * 2,
        scratch_shapes=[pltpu.VMEM((length + 8, lanes), jnp.float32)],
    )(projected, before, after, w_rise, b_rise[:, None, :], w_fall, b_fall[:, None, :])
    return jnp.transpose(rise, (0, 2, 1)), jnp.transpose(fall, (0, 2, 1))


def group_terms(conv, dt_raw, dt_shift, log_rate, skip_heads, falling):
    runs, length = dt_raw.shape[0], dt_raw.shape[1]
    heads = dt_raw.shape[2]
    inner = conv.shape[2] - 2 * NS
    head_size = inner // heads
    values = conv[:, :, :inner].reshape(runs, length, heads, head_size)
    keys_in = conv[:, :, inner : inner + NS]
    reads = conv[:, :, inner + NS :]
    step = jax.nn.softplus(dt_raw.astype(jnp.float32) + dt_shift[:, None, :])
    rate = -jnp.exp(log_rate)
    rows = jnp.arange(length)
    if falling:
        keep = rows[:, None] <= rows[None, :]
    else:
        keep = rows[:, None] >= rows[None, :]
    cum = jnp.einsum(
        "ts,rsh->rth",
        keep.astype(jnp.float32),
        step * rate[:, None, :],
        precision=lax.Precision.HIGHEST,
    )
    by_head = jnp.transpose(cum, (0, 2, 1))
    decay = jnp.exp(
        jnp.where(keep[None, None], by_head[:, :, :, None] - by_head[:, :, None, :], -1e30)
    )
    scores = jnp.einsum("rtn,rsn->rts", reads, keys_in, preferred_element_type=jnp.float32)
    mixing = (scores[:, None] * decay).astype(jnp.bfloat16)
    values32 = values.astype(jnp.float32)
    scaled = (values32 * step[..., None]).astype(jnp.bfloat16)
    diagonal = jnp.einsum("rhts,rshp->rthp", mixing, scaled, preferred_element_type=jnp.float32)
    last = cum[:, 0] if falling else cum[:, -1]
    to_end = jnp.exp(last[:, None, :] - cum)
    weighted = (values32 * (step * to_end)[..., None]).astype(jnp.bfloat16)
    block_state = jnp.einsum(
        "rshp,rsn->rhpn", weighted, keys_in, preferred_element_type=jnp.float32
    )
    block_decay = jnp.exp(last)
    message = jnp.concatenate(
        [
            block_state.reshape(runs, heads, head_size * NS),
            jnp.broadcast_to(block_decay[..., None], (runs, heads, DECAY_LANES)),
        ],
        axis=-1,
    )
    local = diagonal + skip_heads[:, None, :, None] * values32
    return local, cum, reads, message


def finish(local, cum, reads, entering):
    entering = entering.reshape(local.shape[0], local.shape[2], local.shape[3], NS)
    product = jnp.einsum(
        "rtn,rhpn->rthp", reads.astype(jnp.float32), entering, precision=lax.Precision.HIGHEST
    )
    return local + product * jnp.exp(cum)[..., None]


def swapped(pair):
    return jnp.concatenate([pair[1:2], pair[0:1]], axis=0)


def body(
    stream, w_gate, w_xbc, w_dt, dt_bias, decay_log, conv_w, conv_b, skip_gain, norm_gain, w_out
):
    length = stream.shape[0]
    rows = jnp.concatenate([stream[:, 0, :], stream[:, 1, :]], axis=0)
    gate = jnp.einsum(
        "rtd,de->ret", rows.reshape(2, length, -1), w_gate, preferred_element_type=jnp.float32
    ).astype(jnp.bfloat16)
    projected = jnp.dot(rows, w_xbc, preferred_element_type=jnp.float32).astype(jnp.bfloat16)
    projected = projected.reshape(2, length, projected.shape[1])
    dt_raw = jnp.dot(rows, w_dt, preferred_element_type=jnp.float32).astype(jnp.bfloat16)
    dt_raw = dt_raw.reshape(2, length, dt_raw.shape[1])
    before = shifted(projected[:, length - (K - 1) :], 1)
    after = shifted(projected[:, : K - 1], -1)
    conv_rise, conv_fall = convolve(
        projected, before, after, conv_w, conv_b, swapped(conv_w), swapped(conv_b)
    )
    rising = group_terms(conv_rise, dt_raw, dt_bias, decay_log, skip_gain, False)
    falling = group_terms(
        conv_fall, dt_raw, swapped(dt_bias), swapped(decay_log), swapped(skip_gain), True
    )
    rising_in = exclusive_chain(rising[3], 1)
    falling_in = exclusive_chain(falling[3], -1)
    combined = finish(*rising[:3], rising_in) + finish(*falling[:3], falling_in)
    heads, head_size = combined.shape[2], combined.shape[3]
    gate_heads = jnp.transpose(
        gate.reshape(2, heads, head_size, length).astype(jnp.float32), (0, 3, 1, 2)
    )
    gated = combined * jax.nn.silu(gate_heads)
    mean_square = jnp.mean(gated * gated, axis=(2, 3), keepdims=True)
    normed = (
        gated * lax.rsqrt(mean_square + 1e-05) * norm_gain.reshape(heads, head_size)
    ).astype(jnp.bfloat16)
    projected_out = jnp.einsum(
        "rthp,hpd->rtd",
        normed,
        w_out.reshape(heads, head_size, w_out.shape[1]),
        preferred_element_type=jnp.float32,
    )
    final_rows = (rows.reshape(2, length, -1).astype(jnp.float32) + projected_out).astype(
        jnp.bfloat16
    )
    return jnp.stack([final_rows[0], final_rows[1]], axis=1)


def solution(mesh):
    placed = (P(("dp", "ctx"), None, None), P(), P(), P(), P(), P(), P(), P(), P(), P(), P())
    return jax.shard_map(
        body, mesh=mesh, in_specs=placed, out_specs=P(("dp", "ctx"), None, None), check_vma=False
    )
```

```python
import jax
import jax.numpy as jnp
from jax import lax
from jax.experimental import pallas as pl
from jax.experimental.pallas import tpu as pltpu
from jax.sharding import PartitionSpec as P

NS = 64
K = 4
Q = 256
DECAY_LANES = 128


def shifted(value, distance):
    size = lax.axis_size("ctx")
    if abs(distance) >= size:
        return jax.tree.map(jnp.zeros_like, value)
    if distance > 0:
        pairs = [(i, i + distance) for i in range(size - distance)]
    else:
        pairs = [(i - distance, i) for i in range(size + distance)]
    return lax.ppermute(value, "ctx", pairs)


def combine(earlier, later):
    width = later.shape[-1] - DECAY_LANES
    lanes = lax.broadcasted_iota(jnp.int32, later.shape, later.ndim - 1)
    return later[..., width : width + 1] * earlier + jnp.where(lanes < width, later, 0.0)


def exclusive_chain(element, sense):
    size = lax.axis_size("ctx")
    group = 4
    assert size == group * group
    here = lax.axis_index("ctx")
    spot = here if sense == 1 else size - 1 - here
    slot = spot % group

    def place(position):
        return position if sense == 1 else size - 1 - position

    def send(value, moves):
        pairs = [(place(a), place(b)) for a, b in moves]
        moved = lax.ppermute(value.astype(jnp.bfloat16), "ctx", pairs)
        return moved.astype(jnp.float32)

    tops = range(0, size, group)
    first = send(element, [(t + k, t + k + 1) for t in tops for k in (0, 2)])
    pair = combine(first, element)
    other = send(pair, [(t + a, t + b) for t in tops for a, b in ((1, 3), (3, 1))])
    whole = jnp.where(slot == 1, combine(pair, other), combine(other, pair))
    ends = [t + k for t in tops for k in (1, 3)]
    previous = send(whole, [(a, a + group) for a in ends if a + group < size])
    two = combine(previous, whole)
    further = send(two, [(a, a + 2 * group) for a in ends if a + 2 * group < size])
    entering = combine(further, previous)
    handed = jnp.where(slot == 1, entering, combine(entering, other))
    below = send(handed, [(t + k + 1, t + k) for t in tops for k in (0, 2)])
    chained = jnp.where(slot % 2 == 1, combine(handed, first), below)
    return chained[..., : chained.shape[-1] - DECAY_LANES]


def conv_kernel(x_ref, before_ref, after_ref, wr_ref, br_ref, wf_ref, bf_ref, rise_ref, fall_ref, pad):
    length = x_ref.shape[1]
    x = x_ref[0].astype(jnp.float32)
    pad[pl.ds(0, K - 1), :] = before_ref[0].astype(jnp.float32)
    pad[pl.ds(K - 1, length), :] = x
    total = br_ref[0] + wr_ref[0, 0:1, :] * pad[pl.ds(0, length), :]
    for k in range(1, K):
        total = total + wr_ref[0, k : k + 1, :] * pad[pl.ds(k, length), :]
    rise_ref[0] = jnp.transpose(jax.nn.silu(total)).astype(rise_ref.dtype)
    pad[pl.ds(0, length), :] = x
    pad[pl.ds(length, K - 1), :] = after_ref[0].astype(jnp.float32)
    total = bf_ref[0] + wf_ref[0, 0:1, :] * pad[pl.ds(K - 1, length), :]
    for k in range(1, K):
        total = total + wf_ref[0, k : k + 1, :] * pad[pl.ds(K - 1 - k, length), :]
    fall_ref[0] = jnp.transpose(jax.nn.silu(total)).astype(fall_ref.dtype)


def convolve(projected, before, after, w_rise, b_rise, w_fall, b_fall):
    runs, length, channels = projected.shape
    lanes = channels
    grid = (runs, channels // lanes)
    rows = lambda r, c: (r, 0, c)
    out_spec = pl.BlockSpec((1, lanes, length), lambda r, c: (r, c, 0))
    rise, fall = pl.pallas_call(
        conv_kernel,
        grid=grid,
        in_specs=[
            pl.BlockSpec((1, length, lanes), rows),
            pl.BlockSpec((1, K - 1, lanes), rows),
            pl.BlockSpec((1, K - 1, lanes), rows),
            pl.BlockSpec((1, K, lanes), rows),
            pl.BlockSpec((1, 1, lanes), rows),
            pl.BlockSpec((1, K, lanes), rows),
            pl.BlockSpec((1, 1, lanes), rows),
        ],
        out_specs=[out_spec, out_spec],
        out_shape=[jax.ShapeDtypeStruct((runs, channels, length), jnp.bfloat16)] * 2,
        scratch_shapes=[pltpu.VMEM((length + 8, lanes), jnp.float32)],
    )(projected, before, after, w_rise, b_rise[:, None, :], w_fall, b_fall[:, None, :])
    return jnp.transpose(rise, (0, 2, 1)), jnp.transpose(fall, (0, 2, 1))


def group_terms(conv, dt_raw, dt_shift, log_rate, skip_heads, falling):
    runs, length = dt_raw.shape[0], dt_raw.shape[1]
    heads = dt_raw.shape[2]
    inner = conv.shape[2] - 2 * NS
    head_size = inner // heads
    values = conv[:, :, :inner].reshape(runs, length, heads, head_size)
    keys_in = conv[:, :, inner : inner + NS]
    reads = conv[:, :, inner + NS :]
    step = jax.nn.softplus(dt_raw.astype(jnp.float32) + dt_shift[:, None, :])
    rate = -jnp.exp(log_rate)
    rows = jnp.arange(length)
    if falling:
        keep = rows[:, None] <= rows[None, :]
    else:
        keep = rows[:, None] >= rows[None, :]
    cum = jnp.einsum(
        "ts,rsh->rth",
        keep.astype(jnp.float32),
        step * rate[:, None, :],
        precision=lax.Precision.HIGHEST,
    )
    by_head = jnp.transpose(cum, (0, 2, 1))
    decay = jnp.exp(
        jnp.where(keep[None, None], by_head[:, :, :, None] - by_head[:, :, None, :], -1e30)
    )
    scores = jnp.einsum("rtn,rsn->rts", reads, keys_in, preferred_element_type=jnp.float32)
    mixing = (scores[:, None] * decay).astype(jnp.bfloat16)
    values32 = values.astype(jnp.float32)
    scaled = (values32 * step[..., None]).astype(jnp.bfloat16)
    diagonal = jnp.einsum("rhts,rshp->rthp", mixing, scaled, preferred_element_type=jnp.float32)
    last = cum[:, 0] if falling else cum[:, -1]
    to_end = jnp.exp(last[:, None, :] - cum)
    weighted = (values32 * (step * to_end)[..., None]).astype(jnp.bfloat16)
    block_state = jnp.einsum(
        "rshp,rsn->rhpn", weighted, keys_in, preferred_element_type=jnp.float32
    )
    block_decay = jnp.exp(last)
    message = jnp.concatenate(
        [
            block_state.reshape(runs, heads, head_size * NS),
            jnp.broadcast_to(block_decay[..., None], (runs, heads, DECAY_LANES)),
        ],
        axis=-1,
    )
    local = diagonal + skip_heads[:, None, :, None] * values32
    return local, cum, reads, message


def finish(local, cum, reads, entering):
    entering = entering.reshape(local.shape[0], local.shape[2], local.shape[3], NS)
    product = jnp.einsum(
        "rtn,rhpn->rthp", reads.astype(jnp.float32), entering, precision=lax.Precision.HIGHEST
    )
    return local + product * jnp.exp(cum)[..., None]


def swapped(pair):
    return jnp.concatenate([pair[1:2], pair[0:1]], axis=0)


def body(
    stream, w_gate, w_xbc, w_dt, dt_bias, decay_log, conv_w, conv_b, skip_gain, norm_gain, w_out
):
    length = stream.shape[0]
    rows = jnp.concatenate([stream[:, 0, :], stream[:, 1, :]], axis=0)
    gate = jnp.einsum(
        "rtd,de->ret", rows.reshape(2, length, -1), w_gate, preferred_element_type=jnp.float32
    ).astype(jnp.bfloat16)
    projected = jnp.dot(rows, w_xbc, preferred_element_type=jnp.float32).astype(jnp.bfloat16)
    projected = projected.reshape(2, length, projected.shape[1])
    dt_raw = jnp.dot(rows, w_dt, preferred_element_type=jnp.float32).astype(jnp.bfloat16)
    dt_raw = dt_raw.reshape(2, length, dt_raw.shape[1])
    before = shifted(projected[:, length - (K - 1) :], 1)
    after = shifted(projected[:, : K - 1], -1)
    conv_rise, conv_fall = convolve(
        projected, before, after, conv_w, conv_b, swapped(conv_w), swapped(conv_b)
    )
    rising = group_terms(conv_rise, dt_raw, dt_bias, decay_log, skip_gain, False)
    falling = group_terms(
        conv_fall, dt_raw, swapped(dt_bias), swapped(decay_log), swapped(skip_gain), True
    )
    rising_in = exclusive_chain(rising[3], 1)
    falling_in = exclusive_chain(falling[3], -1)
    combined = finish(*rising[:3], rising_in) + finish(*falling[:3], falling_in)
    heads, head_size = combined.shape[2], combined.shape[3]
    gate_heads = jnp.transpose(
        gate.reshape(2, heads, head_size, length).astype(jnp.float32), (0, 3, 1, 2)
    )
    gated = combined * jax.nn.silu(gate_heads)
    mean_square = jnp.mean(gated * gated, axis=(2, 3), keepdims=True)
    normed = (
        gated * lax.rsqrt(mean_square + 1e-05) * norm_gain.reshape(heads, head_size)
    ).astype(jnp.bfloat16)
    projected_out = jnp.einsum(
        "rthp,hpd->rtd",
        normed,
        w_out.reshape(heads, head_size, w_out.shape[1]),
        preferred_element_type=jnp.float32,
    )
    final_rows = (rows.reshape(2, length, -1).astype(jnp.float32) + projected_out).astype(
        jnp.bfloat16
    )
    return jnp.stack([final_rows[0], final_rows[1]], axis=1)


def solution(mesh):
    placed = (P(("dp", "ctx"), None, None), P(), P(), P(), P(), P(), P(), P(), P(), P(), P())
    return jax.shard_map(
        body, mesh=mesh, in_specs=placed, out_specs=P(("dp", "ctx"), None, None), check_vma=False
    )
```

```python
import jax
import jax.numpy as jnp
from jax import lax
from jax.experimental import pallas as pl
from jax.experimental.pallas import tpu as pltpu
from jax.sharding import PartitionSpec as P

NS = 64
K = 4
Q = 256
DECAY_LANES = 128


def shifted(value, distance):
    size = lax.axis_size("ctx")
    if abs(distance) >= size:
        return jax.tree.map(jnp.zeros_like, value)
    if distance > 0:
        pairs = [(i, i + distance) for i in range(size - distance)]
    else:
        pairs = [(i - distance, i) for i in range(size + distance)]
    return lax.ppermute(value, "ctx", pairs)


def combine(earlier, later):
    width = later.shape[-1] - DECAY_LANES
    lanes = lax.broadcasted_iota(jnp.int32, later.shape, later.ndim - 1)
    return later[..., width : width + 1] * earlier + jnp.where(lanes < width, later, 0.0)


def exclusive_chain(element, sense):
    size = lax.axis_size("ctx")
    group = 4
    assert size == group * group
    here = lax.axis_index("ctx")
    spot = here if sense == 1 else size - 1 - here
    slot = spot % group

    def place(position):
        return position if sense == 1 else size - 1 - position

    def send(value, moves):
        pairs = [(place(a), place(b)) for a, b in moves]
        moved = lax.ppermute(value.astype(jnp.bfloat16), "ctx", pairs)
        return moved.astype(jnp.float32)

    tops = range(0, size, group)
    first = send(element, [(t + k, t + k + 1) for t in tops for k in (0, 2)])
    pair = combine(first, element)
    other = send(pair, [(t + a, t + b) for t in tops for a, b in ((1, 3), (3, 1))])
    whole = jnp.where(slot == 1, combine(pair, other), combine(other, pair))
    ends = [t + k for t in tops for k in (1, 3)]
    previous = send(whole, [(a, a + group) for a in ends if a + group < size])
    two = combine(previous, whole)
    further = send(two, [(a, a + 2 * group) for a in ends if a + 2 * group < size])
    entering = combine(further, previous)
    handed = jnp.where(slot == 1, entering, combine(entering, other))
    below = send(handed, [(t + k + 1, t + k) for t in tops for k in (0, 2)])
    chained = jnp.where(slot % 2 == 1, combine(handed, first), below)
    return chained[..., : chained.shape[-1] - DECAY_LANES]


def conv_kernel(x_ref, before_ref, after_ref, wr_ref, br_ref, wf_ref, bf_ref, rise_ref, fall_ref, pad):
    length = x_ref.shape[1]
    x = x_ref[0].astype(jnp.float32)
    pad[pl.ds(0, K - 1), :] = before_ref[0].astype(jnp.float32)
    pad[pl.ds(K - 1, length), :] = x
    total = br_ref[0] + wr_ref[0, 0:1, :] * pad[pl.ds(0, length), :]
    for k in range(1, K):
        total = total + wr_ref[0, k : k + 1, :] * pad[pl.ds(k, length), :]
    rise_ref[0] = jnp.transpose(jax.nn.silu(total)).astype(rise_ref.dtype)
    pad[pl.ds(0, length), :] = x
    pad[pl.ds(length, K - 1), :] = after_ref[0].astype(jnp.float32)
    total = bf_ref[0] + wf_ref[0, 0:1, :] * pad[pl.ds(K - 1, length), :]
    for k in range(1, K):
        total = total + wf_ref[0, k : k + 1, :] * pad[pl.ds(K - 1 - k, length), :]
    fall_ref[0] = jnp.transpose(jax.nn.silu(total)).astype(fall_ref.dtype)


def convolve(projected, before, after, w_rise, b_rise, w_fall, b_fall):
    runs, length, channels = projected.shape
    lanes = channels
    grid = (runs, channels // lanes)
    rows = lambda r, c: (r, 0, c)
    out_spec = pl.BlockSpec((1, lanes, length), lambda r, c: (r, c, 0))
    rise, fall = pl.pallas_call(
        conv_kernel,
        grid=grid,
        in_specs=[
            pl.BlockSpec((1, length, lanes), rows),
            pl.BlockSpec((1, K - 1, lanes), rows),
            pl.BlockSpec((1, K - 1, lanes), rows),
            pl.BlockSpec((1, K, lanes), rows),
            pl.BlockSpec((1, 1, lanes), rows),
            pl.BlockSpec((1, K, lanes), rows),
            pl.BlockSpec((1, 1, lanes), rows),
        ],
        out_specs=[out_spec, out_spec],
        out_shape=[jax.ShapeDtypeStruct((runs, channels, length), jnp.bfloat16)] * 2,
        scratch_shapes=[pltpu.VMEM((length + 8, lanes), jnp.float32)],
    )(projected, before, after, w_rise, b_rise[:, None, :], w_fall, b_fall[:, None, :])
    return jnp.transpose(rise, (0, 2, 1)), jnp.transpose(fall, (0, 2, 1))


def group_terms(conv, dt_raw, dt_shift, log_rate, skip_heads, falling):
    runs, length = dt_raw.shape[0], dt_raw.shape[1]
    heads = dt_raw.shape[2]
    inner = conv.shape[2] - 2 * NS
    head_size = inner // heads
    values = conv[:, :, :inner].reshape(runs, length, heads, head_size)
    keys_in = conv[:, :, inner : inner + NS]
    reads = conv[:, :, inner + NS :]
    step = jax.nn.softplus(dt_raw.astype(jnp.float32) + dt_shift[:, None, :])
    rate = -jnp.exp(log_rate)
    rows = jnp.arange(length)
    if falling:
        keep = rows[:, None] <= rows[None, :]
    else:
        keep = rows[:, None] >= rows[None, :]
    cum = jnp.einsum(
        "ts,rsh->rth",
        keep.astype(jnp.float32),
        step * rate[:, None, :],
        precision=lax.Precision.HIGHEST,
    )
    by_head = jnp.transpose(cum, (0, 2, 1))
    decay = jnp.exp(
        jnp.where(keep[None, None], by_head[:, :, :, None] - by_head[:, :, None, :], -1e30)
    )
    scores = jnp.einsum("rtn,rsn->rts", reads, keys_in, preferred_element_type=jnp.float32)
    mixing = (scores[:, None] * decay).astype(jnp.bfloat16)
    values32 = values.astype(jnp.float32)
    scaled = (values32 * step[..., None]).astype(jnp.bfloat16)
    diagonal = jnp.einsum("rhts,rshp->rthp", mixing, scaled, preferred_element_type=jnp.float32)
    last = cum[:, 0] if falling else cum[:, -1]
    to_end = jnp.exp(last[:, None, :] - cum)
    weighted = (values32 * (step * to_end)[..., None]).astype(jnp.bfloat16)
    block_state = jnp.einsum(
        "rshp,rsn->rhpn", weighted, keys_in, preferred_element_type=jnp.float32
    )
    block_decay = jnp.exp(last)
    message = jnp.concatenate(
        [
            block_state.reshape(runs, heads, head_size * NS),
            jnp.broadcast_to(block_decay[..., None], (runs, heads, DECAY_LANES)),
        ],
        axis=-1,
    )
    local = diagonal + skip_heads[:, None, :, None] * values32
    return local, cum, reads, message


def finish(local, cum, reads, entering):
    entering = entering.reshape(local.shape[0], local.shape[2], local.shape[3], NS)
    high = entering.astype(jnp.bfloat16)
    low = (entering - high.astype(jnp.float32)).astype(jnp.bfloat16)
    product = jnp.einsum(
        "rtn,rhpn->rthp", reads, high, preferred_element_type=jnp.float32
    ) + jnp.einsum("rtn,rhpn->rthp", reads, low, preferred_element_type=jnp.float32)
    return local + product * jnp.exp(cum)[..., None]


def swapped(pair):
    return jnp.concatenate([pair[1:2], pair[0:1]], axis=0)


def body(
    stream, w_gate, w_xbc, w_dt, dt_bias, decay_log, conv_w, conv_b, skip_gain, norm_gain, w_out
):
    length = stream.shape[0]
    rows = jnp.concatenate([stream[:, 0, :], stream[:, 1, :]], axis=0)
    gate = jnp.einsum(
        "rtd,de->ret", rows.reshape(2, length, -1), w_gate, preferred_element_type=jnp.float32
    ).astype(jnp.bfloat16)
    projected = jnp.dot(rows, w_xbc, preferred_element_type=jnp.float32).astype(jnp.bfloat16)
    projected = projected.reshape(2, length, projected.shape[1])
    dt_raw = jnp.dot(rows, w_dt, preferred_element_type=jnp.float32).astype(jnp.bfloat16)
    dt_raw = dt_raw.reshape(2, length, dt_raw.shape[1])
    before = shifted(projected[:, length - (K - 1) :], 1)
    after = shifted(projected[:, : K - 1], -1)
    conv_rise, conv_fall = convolve(
        projected, before, after, conv_w, conv_b, swapped(conv_w), swapped(conv_b)
    )
    rising = group_terms(conv_rise, dt_raw, dt_bias, decay_log, skip_gain, False)
    falling = group_terms(
        conv_fall, dt_raw, swapped(dt_bias), swapped(decay_log), swapped(skip_gain), True
    )
    rising_in = exclusive_chain(rising[3], 1)
    falling_in = exclusive_chain(falling[3], -1)
    combined = finish(*rising[:3], rising_in) + finish(*falling[:3], falling_in)
    heads, head_size = combined.shape[2], combined.shape[3]
    gate_heads = jnp.transpose(
        gate.reshape(2, heads, head_size, length).astype(jnp.float32), (0, 3, 1, 2)
    )
    gated = combined * jax.nn.silu(gate_heads)
    mean_square = jnp.mean(gated * gated, axis=(2, 3), keepdims=True)
    normed = (
        gated * lax.rsqrt(mean_square + 1e-05) * norm_gain.reshape(heads, head_size)
    ).astype(jnp.bfloat16)
    projected_out = jnp.einsum(
        "rthp,hpd->rtd",
        normed,
        w_out.reshape(heads, head_size, w_out.shape[1]),
        preferred_element_type=jnp.float32,
    )
    final_rows = (rows.reshape(2, length, -1).astype(jnp.float32) + projected_out).astype(
        jnp.bfloat16
    )
    return jnp.stack([final_rows[0], final_rows[1]], axis=1)


def solution(mesh):
    placed = (P(("dp", "ctx"), None, None), P(), P(), P(), P(), P(), P(), P(), P(), P(), P())
    return jax.shard_map(
        body, mesh=mesh, in_specs=placed, out_specs=P(("dp", "ctx"), None, None), check_vma=False
    )
```

```python
import jax
import jax.numpy as jnp
from jax import lax
from jax.experimental import pallas as pl
from jax.experimental.pallas import tpu as pltpu
from jax.sharding import PartitionSpec as P

NS = 64
K = 4
DECAY_LANES = 128


def shifted(value, distance):
    size = lax.axis_size("ctx")
    if abs(distance) >= size:
        return jax.tree.map(jnp.zeros_like, value)
    if distance > 0:
        pairs = [(i, i + distance) for i in range(size - distance)]
    else:
        pairs = [(i - distance, i) for i in range(size + distance)]
    return lax.ppermute(value, "ctx", pairs)


def combine(earlier, later):
    width = later.shape[-1] - DECAY_LANES
    lanes = lax.broadcasted_iota(jnp.int32, later.shape, later.ndim - 1)
    return later[..., width : width + 1] * earlier + jnp.where(lanes < width, later, 0.0)


def exclusive_chain(element, sense):
    size = lax.axis_size("ctx")
    group = 4
    assert size == group * group
    here = lax.axis_index("ctx")
    spot = here if sense == 1 else size - 1 - here
    slot = spot % group

    def place(position):
        return position if sense == 1 else size - 1 - position

    def send(value, moves):
        pairs = [(place(a), place(b)) for a, b in moves]
        moved = lax.ppermute(value.astype(jnp.bfloat16), "ctx", pairs)
        return moved.astype(jnp.float32)

    tops = range(0, size, group)
    first = send(element, [(t + k, t + k + 1) for t in tops for k in (0, 2)])
    pair = combine(first, element)
    other = send(pair, [(t + a, t + b) for t in tops for a, b in ((1, 3), (3, 1))])
    whole = jnp.where(slot == 1, combine(pair, other), combine(other, pair))
    ends = [t + k for t in tops for k in (1, 3)]
    previous = send(whole, [(a, a + group) for a in ends if a + group < size])
    two = combine(previous, whole)
    further = send(two, [(a, a + 2 * group) for a in ends if a + 2 * group < size])
    entering = combine(further, previous)
    handed = jnp.where(slot == 1, entering, combine(entering, other))
    below = send(handed, [(t + k + 1, t + k) for t in tops for k in (0, 2)])
    chained = jnp.where(slot % 2 == 1, combine(handed, first), below)
    return chained[..., : chained.shape[-1] - DECAY_LANES]


def conv_kernel(x_ref, before_ref, after_ref, wr_ref, br_ref, wf_ref, bf_ref, rise_ref, fall_ref, pad):
    length = x_ref.shape[1]
    x = x_ref[0].astype(jnp.float32)
    pad[pl.ds(0, K - 1), :] = before_ref[0].astype(jnp.float32)
    pad[pl.ds(K - 1, length), :] = x
    total = br_ref[0] + wr_ref[0, 0:1, :] * pad[pl.ds(0, length), :]
    for k in range(1, K):
        total = total + wr_ref[0, k : k + 1, :] * pad[pl.ds(k, length), :]
    rise_ref[0] = jnp.transpose(jax.nn.silu(total)).astype(rise_ref.dtype)
    pad[pl.ds(0, length), :] = x
    pad[pl.ds(length, K - 1), :] = after_ref[0].astype(jnp.float32)
    total = bf_ref[0] + wf_ref[0, 0:1, :] * pad[pl.ds(K - 1, length), :]
    for k in range(1, K):
        total = total + wf_ref[0, k : k + 1, :] * pad[pl.ds(K - 1 - k, length), :]
    fall_ref[0] = jnp.transpose(jax.nn.silu(total)).astype(fall_ref.dtype)


def convolve(projected, before, after, w_rise, b_rise, w_fall, b_fall):
    runs, length, channels = projected.shape
    lanes = channels
    grid = (runs, channels // lanes)
    rows = lambda r, c: (r, 0, c)
    out_spec = pl.BlockSpec((1, lanes, length), lambda r, c: (r, c, 0))
    rise, fall = pl.pallas_call(
        conv_kernel,
        grid=grid,
        in_specs=[
            pl.BlockSpec((1, length, lanes), rows),
            pl.BlockSpec((1, K - 1, lanes), rows),
            pl.BlockSpec((1, K - 1, lanes), rows),
            pl.BlockSpec((1, K, lanes), rows),
            pl.BlockSpec((1, 1, lanes), rows),
            pl.BlockSpec((1, K, lanes), rows),
            pl.BlockSpec((1, 1, lanes), rows),
        ],
        out_specs=[out_spec, out_spec],
        out_shape=[jax.ShapeDtypeStruct((runs, channels, length), jnp.bfloat16)] * 2,
        scratch_shapes=[pltpu.VMEM((length + 8, lanes), jnp.float32)],
    )(projected, before, after, w_rise, b_rise[:, None, :], w_fall, b_fall[:, None, :])
    return jnp.transpose(rise, (0, 2, 1)), jnp.transpose(fall, (0, 2, 1))


def group_terms(conv, dt_raw, dt_shift, log_rate, skip_heads, falling):
    runs, length = dt_raw.shape[0], dt_raw.shape[1]
    heads = dt_raw.shape[2]
    inner = conv.shape[2] - 2 * NS
    head_size = inner // heads
    values = conv[:, :, :inner].reshape(runs, length, heads, head_size)
    keys_in = conv[:, :, inner : inner + NS]
    reads = conv[:, :, inner + NS :]
    step = jax.nn.softplus(dt_raw.astype(jnp.float32) + dt_shift[:, None, :])
    rate = -jnp.exp(log_rate)
    rows = jnp.arange(length)
    if falling:
        keep = rows[:, None] <= rows[None, :]
    else:
        keep = rows[:, None] >= rows[None, :]
    cum = jnp.einsum(
        "ts,rsh->rth",
        keep.astype(jnp.float32),
        step * rate[:, None, :],
        precision=lax.Precision.HIGHEST,
    )
    by_head = jnp.transpose(cum, (0, 2, 1))
    decay = jnp.exp(
        jnp.where(keep[None, None], by_head[:, :, :, None] - by_head[:, :, None, :], -1e30)
    )
    scores = jnp.einsum("rtn,rsn->rts", reads, keys_in, preferred_element_type=jnp.float32)
    mixing = (scores[:, None] * decay).astype(jnp.bfloat16)
    values32 = values.astype(jnp.float32)
    scaled = (values32 * step[..., None]).astype(jnp.bfloat16)
    diagonal = jnp.einsum(
        "rhts,rshp->rthp", mixing, scaled, preferred_element_type=jnp.float32
    )
    last = cum[:, 0] if falling else cum[:, -1]
    to_end = jnp.exp(last[:, None, :] - cum)
    weighted = (values32 * (step * to_end)[..., None]).astype(jnp.bfloat16)
    block_state = jnp.einsum(
        "rshp,rsn->rhpn", weighted, keys_in, preferred_element_type=jnp.float32
    )
    block_decay = jnp.exp(last)
    message = jnp.concatenate(
        [
            block_state.reshape(runs, heads, head_size * NS),
            jnp.broadcast_to(block_decay[..., None], (runs, heads, DECAY_LANES)),
        ],
        axis=-1,
    )
    local = diagonal + skip_heads[:, None, :, None] * values32
    return local, cum, reads, message


def finish(local, cum, reads, entering):
    entering = entering.reshape(local.shape[0], local.shape[2], local.shape[3], NS)
    product = jnp.einsum(
        "rtn,rhpn->rthp", reads.astype(jnp.float32), entering, precision=lax.Precision.HIGHEST
    )
    return local + product * jnp.exp(cum)[..., None]


def swapped(pair):
    return jnp.concatenate([pair[1:2], pair[0:1]], axis=0)


def body(
    stream, w_gate, w_xbc, w_dt, dt_bias, decay_log, conv_w, conv_b, skip_gain, norm_gain, w_out
):
    length = stream.shape[0]
    rows = jnp.concatenate([stream[:, 0, :], stream[:, 1, :]], axis=0)
    gate = jnp.einsum(
        "rtd,de->ret", rows.reshape(2, length, -1), w_gate, preferred_element_type=jnp.float32
    ).astype(jnp.bfloat16)
    projected = jnp.dot(rows, w_xbc, preferred_element_type=jnp.float32).astype(jnp.bfloat16)
    projected = projected.reshape(2, length, projected.shape[1])
    dt_raw = jnp.dot(rows, w_dt, preferred_element_type=jnp.float32).astype(jnp.bfloat16)
    dt_raw = dt_raw.reshape(2, length, dt_raw.shape[1])
    before = shifted(projected[:, length - (K - 1) :], 1)
    after = shifted(projected[:, : K - 1], -1)
    conv_rise, conv_fall = convolve(
        projected, before, after, conv_w, conv_b, swapped(conv_w), swapped(conv_b)
    )
    rising = group_terms(conv_rise, dt_raw, dt_bias, decay_log, skip_gain, False)
    falling = group_terms(
        conv_fall, dt_raw, swapped(dt_bias), swapped(decay_log), swapped(skip_gain), True
    )
    rising_in = exclusive_chain(rising[3], 1)
    falling_in = exclusive_chain(falling[3], -1)
    combined = finish(*rising[:3], rising_in) + finish(*falling[:3], falling_in)
    heads, head_size = combined.shape[2], combined.shape[3]
    gate_heads = jnp.transpose(
        gate.reshape(2, heads, head_size, length).astype(jnp.float32), (0, 3, 1, 2)
    )
    gated = combined * jax.nn.silu(gate_heads)
    mean_square = jnp.mean(gated * gated, axis=(2, 3), keepdims=True)
    normed = (
        gated * lax.rsqrt(mean_square + 1e-05) * norm_gain.reshape(heads, head_size)
    ).astype(jnp.bfloat16)
    projected_out = jnp.einsum(
        "rthp,hpd->rtd",
        normed,
        w_out.reshape(heads, head_size, w_out.shape[1]),
        preferred_element_type=jnp.float32,
    )
    final_rows = (rows.reshape(2, length, -1).astype(jnp.float32) + projected_out).astype(
        jnp.bfloat16
    )
    return jnp.stack([final_rows[0], final_rows[1]], axis=1)


def solution(mesh):
    placed = (P(("dp", "ctx"), None, None), P(), P(), P(), P(), P(), P(), P(), P(), P(), P())

    return jax.shard_map(
        body, mesh=mesh, in_specs=placed, out_specs=P(("dp", "ctx"), None, None), check_vma=False
    )
```

```python
import jax
import jax.numpy as jnp
from jax import lax
from jax.experimental import pallas as pl
from jax.experimental.pallas import tpu as pltpu
from jax.sharding import PartitionSpec as P

NS = 64
K = 4
Q = 256
DECAY_LANES = 128


def shifted(value, distance):
    size = lax.axis_size("ctx")
    if abs(distance) >= size:
        return jax.tree.map(jnp.zeros_like, value)
    if distance > 0:
        pairs = [(i, i + distance) for i in range(size - distance)]
    else:
        pairs = [(i - distance, i) for i in range(size + distance)]
    return lax.ppermute(value, "ctx", pairs)


def combine(earlier, later):
    width = later.shape[-1] - DECAY_LANES
    lanes = lax.broadcasted_iota(jnp.int32, later.shape, later.ndim - 1)
    return later[..., width : width + 1] * earlier + jnp.where(lanes < width, later, 0.0)


def exclusive_chain(element, sense):
    size = lax.axis_size("ctx")
    group = 4
    assert size == group * group
    here = lax.axis_index("ctx")
    spot = here if sense == 1 else size - 1 - here
    slot = spot % group

    def place(position):
        return position if sense == 1 else size - 1 - position

    def send(value, moves):
        pairs = [(place(a), place(b)) for a, b in moves]
        moved = lax.ppermute(value.astype(jnp.bfloat16), "ctx", pairs)
        return moved.astype(jnp.float32)

    tops = range(0, size, group)
    first = send(element, [(t + k, t + k + 1) for t in tops for k in (0, 2)])
    pair = combine(first, element)
    other = send(pair, [(t + a, t + b) for t in tops for a, b in ((1, 3), (3, 1))])
    whole = jnp.where(slot == 1, combine(pair, other), combine(other, pair))
    ends = [t + k for t in tops for k in (1, 3)]
    previous = send(whole, [(a, a + group) for a in ends if a + group < size])
    two = combine(previous, whole)
    further = send(two, [(a, a + 2 * group) for a in ends if a + 2 * group < size])
    entering = combine(further, previous)
    handed = jnp.where(slot == 1, entering, combine(entering, other))
    below = send(handed, [(t + k + 1, t + k) for t in tops for k in (0, 2)])
    chained = jnp.where(slot % 2 == 1, combine(handed, first), below)
    return chained[..., : chained.shape[-1] - DECAY_LANES]


def conv_kernel(x_ref, before_ref, after_ref, wr_ref, br_ref, wf_ref, bf_ref, rise_ref, fall_ref, pad):
    length = x_ref.shape[1]
    x = x_ref[0].astype(jnp.float32)
    pad[pl.ds(0, K - 1), :] = before_ref[0].astype(jnp.float32)
    pad[pl.ds(K - 1, length), :] = x
    total = br_ref[0] + wr_ref[0, 0:1, :] * pad[pl.ds(0, length), :]
    for k in range(1, K):
        total = total + wr_ref[0, k : k + 1, :] * pad[pl.ds(k, length), :]
    rise_ref[0] = jnp.transpose(jax.nn.silu(total)).astype(rise_ref.dtype)
    pad[pl.ds(0, length), :] = x
    pad[pl.ds(length, K - 1), :] = after_ref[0].astype(jnp.float32)
    total = bf_ref[0] + wf_ref[0, 0:1, :] * pad[pl.ds(K - 1, length), :]
    for k in range(1, K):
        total = total + wf_ref[0, k : k + 1, :] * pad[pl.ds(K - 1 - k, length), :]
    fall_ref[0] = jnp.transpose(jax.nn.silu(total)).astype(fall_ref.dtype)


def convolve(projected, before, after, w_rise, b_rise, w_fall, b_fall):
    runs, length, channels = projected.shape
    lanes = channels
    grid = (runs, channels // lanes)
    rows = lambda r, c: (r, 0, c)
    out_spec = pl.BlockSpec((1, lanes, length), lambda r, c: (r, c, 0))
    rise, fall = pl.pallas_call(
        conv_kernel,
        grid=grid,
        in_specs=[
            pl.BlockSpec((1, length, lanes), rows),
            pl.BlockSpec((1, K - 1, lanes), rows),
            pl.BlockSpec((1, K - 1, lanes), rows),
            pl.BlockSpec((1, K, lanes), rows),
            pl.BlockSpec((1, 1, lanes), rows),
            pl.BlockSpec((1, K, lanes), rows),
            pl.BlockSpec((1, 1, lanes), rows),
        ],
        out_specs=[out_spec, out_spec],
        out_shape=[jax.ShapeDtypeStruct((runs, channels, length), jnp.bfloat16)] * 2,
        scratch_shapes=[pltpu.VMEM((length + 8, lanes), jnp.float32)],
    )(projected, before, after, w_rise, b_rise[:, None, :], w_fall, b_fall[:, None, :])
    return jnp.transpose(rise, (0, 2, 1)), jnp.transpose(fall, (0, 2, 1))


def group_terms(conv, dt_raw, dt_shift, log_rate, skip_heads, falling):
    runs, length = dt_raw.shape[0], dt_raw.shape[1]
    heads = dt_raw.shape[2]
    inner = conv.shape[2] - 2 * NS
    head_size = inner // heads
    values = conv[:, :, :inner].reshape(runs, length, heads, head_size)
    keys_in = conv[:, :, inner : inner + NS]
    reads = conv[:, :, inner + NS :]
    step = jax.nn.softplus(dt_raw.astype(jnp.float32) + dt_shift[:, None, :])
    rate = -jnp.exp(log_rate)
    rows = jnp.arange(length)
    if falling:
        keep = rows[:, None] <= rows[None, :]
    else:
        keep = rows[:, None] >= rows[None, :]
    cum = jnp.einsum(
        "ts,rsh->rth",
        keep.astype(jnp.float32),
        step * rate[:, None, :],
        precision=lax.Precision.HIGHEST,
    )
    by_head = jnp.transpose(cum, (0, 2, 1))
    decay = jnp.exp(
        jnp.where(keep[None, None], by_head[:, :, :, None] - by_head[:, :, None, :], -1e30)
    )
    scores = jnp.einsum("rtn,rsn->rts", reads, keys_in, preferred_element_type=jnp.float32)
    mixing = (scores[:, None] * decay).astype(jnp.bfloat16)
    values32 = values.astype(jnp.float32)
    scaled = (values32 * step[..., None]).astype(jnp.bfloat16)
    diagonal = jnp.einsum("rhts,rshp->rthp", mixing, scaled, preferred_element_type=jnp.float32)
    last = cum[:, 0] if falling else cum[:, -1]
    to_end = jnp.exp(last[:, None, :] - cum)
    weighted = (values32 * (step * to_end)[..., None]).astype(jnp.bfloat16)
    block_state = jnp.einsum(
        "rshp,rsn->rhpn", weighted, keys_in, preferred_element_type=jnp.float32
    )
    block_decay = jnp.exp(last)
    message = jnp.concatenate(
        [
            block_state.reshape(runs, heads, head_size * NS),
            jnp.broadcast_to(block_decay[..., None], (runs, heads, DECAY_LANES)),
        ],
        axis=-1,
    )
    local = diagonal + skip_heads[:, None, :, None] * values32
    return local, cum, reads, message


def finish(local, cum, reads, entering):
    entering = entering.reshape(local.shape[0], local.shape[2], local.shape[3], NS)
    product = jnp.einsum(
        "rtn,rhpn->rthp", reads.astype(jnp.float32), entering, precision=lax.Precision.HIGH
    )
    return local + product * jnp.exp(cum)[..., None]


def swapped(pair):
    return jnp.concatenate([pair[1:2], pair[0:1]], axis=0)


def body(
    stream, w_gate, w_xbc, w_dt, dt_bias, decay_log, conv_w, conv_b, skip_gain, norm_gain, w_out
):
    length = stream.shape[0]
    rows = jnp.concatenate([stream[:, 0, :], stream[:, 1, :]], axis=0)
    gate = jnp.einsum(
        "rtd,de->ret", rows.reshape(2, length, -1), w_gate, preferred_element_type=jnp.float32
    ).astype(jnp.bfloat16)
    projected = jnp.dot(rows, w_xbc, preferred_element_type=jnp.float32).astype(jnp.bfloat16)
    projected = projected.reshape(2, length, projected.shape[1])
    dt_raw = jnp.dot(rows, w_dt, preferred_element_type=jnp.float32).astype(jnp.bfloat16)
    dt_raw = dt_raw.reshape(2, length, dt_raw.shape[1])
    before = shifted(projected[:, length - (K - 1) :], 1)
    after = shifted(projected[:, : K - 1], -1)
    conv_rise, conv_fall = convolve(
        projected, before, after, conv_w, conv_b, swapped(conv_w), swapped(conv_b)
    )
    rising = group_terms(conv_rise, dt_raw, dt_bias, decay_log, skip_gain, False)
    falling = group_terms(
        conv_fall, dt_raw, swapped(dt_bias), swapped(decay_log), swapped(skip_gain), True
    )
    rising_in = exclusive_chain(rising[3], 1)
    falling_in = exclusive_chain(falling[3], -1)
    combined = finish(*rising[:3], rising_in) + finish(*falling[:3], falling_in)
    heads, head_size = combined.shape[2], combined.shape[3]
    gate_heads = jnp.transpose(
        gate.reshape(2, heads, head_size, length).astype(jnp.float32), (0, 3, 1, 2)
    )
    gated = combined * jax.nn.silu(gate_heads)
    mean_square = jnp.mean(gated * gated, axis=(2, 3), keepdims=True)
    normed = (
        gated * lax.rsqrt(mean_square + 1e-05) * norm_gain.reshape(heads, head_size)
    ).astype(jnp.bfloat16)
    projected_out = jnp.einsum(
        "rthp,hpd->rtd",
        normed,
        w_out.reshape(heads, head_size, w_out.shape[1]),
        preferred_element_type=jnp.float32,
    )
    final_rows = (rows.reshape(2, length, -1).astype(jnp.float32) + projected_out).astype(
        jnp.bfloat16
    )
    return jnp.stack([final_rows[0], final_rows[1]], axis=1)


def solution(mesh):
    placed = (P(("dp", "ctx"), None, None), P(), P(), P(), P(), P(), P(), P(), P(), P(), P())
    return jax.shard_map(
        body, mesh=mesh, in_specs=placed, out_specs=P(("dp", "ctx"), None, None), check_vma=False
    )
```
